32 devices in a mesh: seq: 8 (over y, x, core), head: 4 (over z).
Axes of the slice: x: 2, y: 2, z: 4, core: 2. Of those that a mesh axis runs over, the one named last changes fastest.
Arguments:
- hidden: bfloat16 [4096, 2048], P(('seq', 'head')), may hold values from -41 to 41
- w_qkv: bfloat16 [2048, 3072], replicated, may hold values from -0.125 to 0.125
- w_out: bfloat16 [2048, 2048], replicated, may hold values from -0.125 to 0.125
- seg_ids: int32 [4096], replicated, may hold values from 0 to 7, never falling along the last dimension, each value on 1 to 2048 neighbouring positions
- live: int32 [4096], replicated, may hold values 0 or 1
- page_table: int32 [256], replicated, may hold values from 0 to 255, as said below
Outputs:
- mixed: bfloat16 [4096, 2048], P(('seq', 'head'))
- kv_pool: bfloat16 [8, 256, 16, 128], P('head', 'seq')
The draws below stay inside these ranges and needn't reach their ends.
Inputs may be any that keep to these rules, and one draw needn't show every extreme that they name: `page_table`: A permutation of the 256 pages; pool shard r along seq holds pages r * 32 to (r + 1) * 32 - 1, and the 32 logical pages of each seq group go exactly 4 to each pool shard.
All inputs are finite; a program needn't handle non-finite values.
Results may differ from the reference program's by a relative error of at most 0.0059.
The reference program's roundings to bfloat16 on the way (of `packed`, `weights` and `attended`) count: a program that leaves them out, or rounds other values in their place, can miss the bound.
Values may be sent and summed in bfloat16 or wider, within the bound.
No kernel may reach another device: no remote copies, remote signals or barrier semaphores. Data moves between devices by JAX's collectives and lax.ppermute only.
A program may use at most 128 MiB of HBM per device.

```python
import math
import jax
import jax.numpy as jnp
import numpy as np
from jax import lax

D = 2048
H = 32
KVH = 8
HD = 64
PAGE = 16
SEGS = 8
QPK = 4
QKV = 3072
TOKENS = 4096
GT = 512
MAXLEN = 2048
PAGES = 256
LP_GROUP = 32
SENDS = 4


def draw_hidden(key, part):
    base = jnp.clip(jax.random.normal(jax.random.fold_in(key, 11), (TOKENS, D), jnp.float32), -6.0, 6.0)
    phase = jax.random.uniform(jax.random.fold_in(key, 15), (), jnp.float32, 0.0, 6.2831853)
    direction = jnp.clip(jax.random.normal(jax.random.fold_in(key, 16), (1, D), jnp.float32), -3.0, 3.0)
    place = jnp.arange(TOKENS, dtype=jnp.float32)[:, None] * (6.2831853 / TOKENS)
    drift = 1.5 * jnp.cos(place + phase) * direction
    sign = jnp.where(jax.random.bernoulli(jax.random.fold_in(key, 17), 0.5, ()), 1.0, -1.0)
    group_of = jnp.arange(TOKENS, dtype=jnp.int32)[:, None] // GT
    alternate = (1 - 2 * (group_of % 2)).astype(jnp.float32)
    drift = drift + 1.5 * sign * alternate * direction
    return jnp.clip(base + drift, -41.0, 41.0).astype(jnp.bfloat16)


def draw_page_table(key, part):
    groups = LP_GROUP // SENDS
    row = jnp.repeat(jnp.arange(groups, dtype=jnp.int32), SENDS)
    dest_keys = jax.random.split(jax.random.fold_in(key, 21), groups)
    dest = jax.vmap(lambda one: jax.random.permutation(one, row))(dest_keys).reshape(PAGES)
    order = jnp.argsort(dest, stable=True)
    sorted_dest = dest[order]
    position = jnp.arange(PAGES, dtype=jnp.int32) % LP_GROUP
    slot_keys = jax.random.split(jax.random.fold_in(key, 22), groups)
    slot_table = jax.vmap(lambda one: jax.random.permutation(one, jnp.arange(LP_GROUP, dtype=jnp.int32)))(slot_keys)
    physical = sorted_dest * LP_GROUP + slot_table[sorted_dest, position]
    return jnp.zeros((PAGES,), jnp.int32).at[order].set(physical.astype(jnp.int32))


def touch_ends(drawn, stream_key, least, high):
    index_at = [jax.random.randint(jax.random.fold_in(stream_key, axis), (), 0, length) for axis, length in enumerate(drawn.shape)]
    longest = drawn.shape.index(max(drawn.shape))
    next_to = index_at[:longest] + [(index_at[longest] + 1) % drawn.shape[longest]] + index_at[longest + 1:]
    return drawn.at[tuple(index_at)].set(least).at[tuple(next_to)].set(high)


def split_up(count, total, most, skew):
    weights = [(1 << 20) // math.isqrt(standing ** skew) + 1 for standing in range(2, count + 1)]
    surplus, given = total - most - (count - 1), [1] * (count - 1)
    while surplus > 0:
        movable = [i for i in range(count - 1) if given[i] < most]
        pool, left = sum([weights[i] for i in movable]), surplus
        for i in movable:
            addition = min(most - given[i], max(1, left * weights[i] // pool), surplus)
            given[i] = given[i] + addition
            surplus = surplus - addition
    return np.array([most] + given)


def ragged_sizes(rng, amount, total, most, slope):
    if amount == 2:
        one = jax.random.randint(rng, (), max(1, total - most), min(most, total - 1) + 1)
        return jnp.stack([one, total - one])
    sizes = jnp.asarray(split_up(amount, total, most, slope), jnp.int32)
    couples = (amount - 1) // 2
    source_of, sink = sizes[1:1 + 2 * couples:2], sizes[2:2 + 2 * couples:2]
    slack = jnp.minimum(source_of - 1, most - sink)
    passed = jax.random.randint(jax.random.fold_in(rng, 1), (couples,), 0, 1 << 20) % (slack + 1)
    sizes = sizes.at[1:1 + 2 * couples:2].set(source_of - passed).at[2:2 + 2 * couples:2].set(sink + passed)
    return sizes[jax.random.permutation(jax.random.fold_in(rng, 2), amount)]


def gaussian(stream_key, shape, width, limit, kind=jnp.bfloat16):
    values = jax.random.normal(stream_key, shape, jnp.float32) * width
    return jnp.minimum(jnp.maximum(values, -limit), limit).astype(kind)


def setup_inputs(seed: int = 0) -> dict:
    key_of = jax.random.split(jax.random.key(seed), 7)
    hidden = draw_hidden(jax.random.fold_in(key_of[6], 71), 0)
    w_qkv = gaussian(key_of[1], (D, QKV), D ** -0.5, 0.125)
    w_out = gaussian(key_of[2], (H * HD, D), (H * HD) ** -0.5, 0.125)
    seg_ids = jnp.searchsorted(jnp.cumsum(ragged_sizes(key_of[3], SEGS, TOKENS, MAXLEN, 0)), jnp.arange(TOKENS), side="right").astype(jnp.int32)
    live = touch_ends((jax.random.randint(key_of[4], (TOKENS,), 0, 16) < 15).astype(jnp.int32), jax.random.fold_in(key_of[4], 1), 0, 1)
    page_table = draw_page_table(jax.random.fold_in(key_of[6], 71), 0)
    return dict(hidden=hidden, w_qkv=w_qkv, w_out=w_out, seg_ids=seg_ids, live=live, page_table=page_table)


def reference(hidden, w_qkv, w_out, seg_ids, live, page_table):
    tokens = hidden.shape[0]
    packed = jnp.dot(hidden, w_qkv, preferred_element_type=jnp.float32).astype(jnp.bfloat16)
    shaped = packed.reshape(tokens, KVH, QPK + 2, HD)
    queries = shaped[:, :, :QPK].astype(jnp.float32)
    keyvals = shaped[:, :, QPK:].reshape(tokens, KVH, 2 * HD)
    keys = keyvals[:, :, :HD].astype(jnp.float32)
    values = keyvals[:, :, HD:].astype(jnp.float32)
    index = jnp.arange(tokens, dtype=jnp.int32)
    block = min(tokens, 512)

    def one_block(number):
        begin = (number * block).astype(jnp.int32)
        q_block = lax.dynamic_slice_in_dim(queries, begin, block, 0)
        q_index = begin + jnp.arange(block, dtype=jnp.int32)
        q_seg = lax.dynamic_slice_in_dim(seg_ids, begin, block, 0)
        allowed = (seg_ids[None, :] == q_seg[:, None]) & (index[None, :] <= q_index[:, None])
        allowed = allowed & ((live[None, :] == 1) | (index[None, :] == q_index[:, None]))

        def one_group(group):
            q_group = lax.dynamic_index_in_dim(q_block, group, 1, keepdims=False)
            k_group = lax.dynamic_index_in_dim(keys, group, 1, keepdims=False)
            v_group = lax.dynamic_index_in_dim(values, group, 1, keepdims=False)
            scores = jnp.einsum("qcd,kd->cqk", q_group, k_group) * 0.015625
            masked = jnp.where(allowed[None], scores, -1e30)
            top = jnp.max(masked, axis=-1, keepdims=True)
            weights = jnp.where(allowed[None], jnp.exp(masked - top), 0.0)
            total = jnp.sum(weights, axis=-1)
            rounded = lax.optimization_barrier(weights.astype(jnp.bfloat16)).astype(jnp.float32)
            return jnp.einsum("cqk,kd->cqd", rounded, v_group) / total[..., None]

        return lax.map(one_group, jnp.arange(KVH, dtype=jnp.int32))

    blocks = lax.map(one_block, jnp.arange(tokens // block, dtype=jnp.int32))
    attended = blocks.transpose(0, 3, 1, 2, 4).reshape(tokens, KVH * QPK * HD).astype(jnp.bfloat16)
    mixed = jnp.dot(attended, w_out, preferred_element_type=jnp.float32).astype(jnp.bfloat16)
    pages = keyvals.reshape(tokens // PAGE, PAGE, KVH, 2 * HD)
    kv_pool = jnp.zeros_like(pages).at[page_table].set(pages)
    return mixed, kv_pool.transpose(2, 0, 1, 3)
```

```python
import math

import jax
import jax.numpy as jnp
from jax import lax
from jax.sharding import PartitionSpec as P

KVH = 8
HD = 64
PAGE = 16
QPK = 4


def shards(hidden, w_qkv, w_out, seg_ids, live, page_table):
    heads_n = lax.axis_size("head")
    head_at = lax.axis_index("head")
    seq_at = lax.axis_index("seq")
    groups_here = KVH // heads_n
    per_group = (QPK + 2) * HD
    columns = groups_here * per_group
    local = jnp.dot(hidden, w_qkv, preferred_element_type=jnp.float32).astype(jnp.bfloat16)
    local = local.reshape(local.shape[0], heads_n, columns)
    grouped = lax.all_to_all(local, "head", split_axis=1, concat_axis=0, tiled=True)
    grouped = grouped.reshape(grouped.shape[0], columns)
    group_rows = grouped.shape[0]
    shaped = grouped.reshape(group_rows, groups_here, QPK + 2, HD)
    queries = shaped[:, :, :QPK]
    keyvals = shaped[:, :, QPK:].reshape(group_rows, groups_here, 2 * HD)
    first_row = seq_at * group_rows
    q_index = first_row + jnp.arange(group_rows, dtype=jnp.int32)
    q_seg = lax.dynamic_slice_in_dim(seg_ids, first_row, group_rows, 0)
    start_max = jnp.full((groups_here, QPK, group_rows), -1e30, jnp.float32)
    start_total = jnp.zeros((groups_here, QPK, group_rows), jnp.float32)
    start_acc = jnp.zeros((groups_here, QPK, group_rows, HD), jnp.float32)
    carry = (start_max, start_total, start_acc)
    piece = lax.all_gather(keyvals, "seq", axis=0, tiled=True)
    rows = piece.shape[0]
    block = math.gcd(rows, 1024)

    def advance(state, number):
        offset = number * block
        kv_block = lax.dynamic_slice_in_dim(piece, offset, block, 0)
        k_index = offset + jnp.arange(block, dtype=jnp.int32)
        k_seg = lax.dynamic_slice_in_dim(seg_ids, offset, block, 0)
        k_live = lax.dynamic_slice_in_dim(live, offset, block, 0)
        active = (offset <= q_index[-1]) & (k_seg[0] <= q_seg[-1]) & (k_seg[-1] >= q_seg[0])

        def compute(inner):
            run_max, run_total, run_acc = inner
            allowed = (k_seg[None, :] == q_seg[:, None]) & (k_index[None, :] <= q_index[:, None])
            allowed = allowed & ((k_live[None, :] == 1) | (k_index[None, :] == q_index[:, None]))
            scores = (
                jnp.einsum(
                    "qgcd,kgd->gcqk",
                    queries,
                    kv_block[:, :, :HD],
                    preferred_element_type=jnp.float32,
                )
                * 0.015625
            )
            masked = jnp.where(allowed[None, None], scores, -1e30)
            new_max = jnp.maximum(run_max, jnp.max(masked, axis=-1))
            weights = jnp.where(allowed[None, None], jnp.exp(masked - new_max[..., None]), 0.0)
            factor = jnp.exp(run_max - new_max)
            new_total = run_total * factor + jnp.sum(weights, axis=-1)
            update = jnp.einsum(
                "gcqk,kgd->gcqd",
                weights.astype(jnp.bfloat16),
                kv_block[:, :, HD:],
                preferred_element_type=jnp.float32,
            )
            return (new_max, new_total, run_acc * factor[..., None] + update)

        return (lax.cond(active, compute, lambda inner: inner, state), None)

    carry, _ = lax.scan(advance, carry, jnp.arange(rows // block, dtype=jnp.int32))
    final_max, final_total, final_acc = carry
    attended = (final_acc / final_total[..., None]).transpose(2, 0, 1, 3)
    attended = attended.reshape(group_rows, groups_here * QPK * HD).astype(jnp.bfloat16)
    own_tokens = lax.all_to_all(attended, "head", split_axis=0, concat_axis=1, tiled=True)
    mixed = jnp.dot(own_tokens, w_out, preferred_element_type=jnp.float32).astype(jnp.bfloat16)
    pages_n = page_table.shape[0]
    page_count = pages_n // lax.axis_size("seq")
    all_pages = piece.reshape(pages_n, PAGE, groups_here, 2 * HD)
    wanted = seq_at * page_count + jnp.arange(page_count, dtype=jnp.int32)
    hits = page_table[None, :] == wanted[:, None]
    logical = jnp.sum(jnp.where(hits, jnp.arange(pages_n, dtype=jnp.int32)[None, :], 0), axis=1)
    kv_pool = jnp.take(all_pages, logical, axis=0).transpose(2, 0, 1, 3)
    return (mixed, kv_pool)


def solution(mesh):
    placed = (P(("seq", "head"), None), P(), P(), P(), P(), P())
    return jax.shard_map(
        shards,
        mesh=mesh,
        in_specs=placed,
        out_specs=(P(("seq", "head"), None), P("head", "seq", None, None)),
        check_vma=False,
    )
```

```python
import functools

import jax
import jax.numpy as jnp
from jax import lax
from jax.experimental import pallas as pl
from jax.experimental.pallas import tpu as pltpu
from jax.sharding import PartitionSpec as P

KVH = 8
HD = 64
PAGE = 16
QPK = 4
TQ = 256
BK = 512
INTERPRET = False


def attention_kernel(seg_sm, base_sm, q_ref, k_ref, v_ref, qseg_ref, qidx_ref, kseg_ref, klive_ref,
                     o_ref, m_sc, l_sc, acc_sc):
    qi = pl.program_id(0)
    ki = pl.program_id(1)
    groups = q_ref.shape[0]
    tq = q_ref.shape[1] // QPK
    bk = k_ref.shape[1]

    @pl.when(ki == 0)
    def _():
        m_sc[...] = jnp.full(m_sc.shape, -1e30, jnp.float32)
        l_sc[...] = jnp.zeros(l_sc.shape, jnp.float32)
        acc_sc[...] = jnp.zeros(acc_sc.shape, jnp.float32)

    q_first = base_sm[0] + qi * tq
    q_last = q_first + tq - 1
    k_first = ki * bk
    k_last = k_first + bk - 1
    active = (k_first <= q_last) & (seg_sm[k_first] <= seg_sm[q_last]) & (seg_sm[k_last] >= seg_sm[q_first])

    @pl.when(active)
    def _():
        kidx = k_first + lax.broadcasted_iota(jnp.int32, (1, bk), 1)
        qidx = qidx_ref[...]
        allowed = (kseg_ref[...] == qseg_ref[...]) & (kidx <= qidx)
        allowed = allowed & ((klive_ref[...] == 1) | (kidx == qidx))
        for g in range(groups):
            scores = lax.dot_general(
                q_ref[g], k_ref[g], (((1,), (1,)), ((), ())), preferred_element_type=jnp.float32
            ) * 0.015625
            masked = jnp.where(allowed, scores, -1e30)
            m_old = m_sc[g]
            m_new = jnp.maximum(m_old, jnp.max(masked, axis=1, keepdims=True))
            weights = jnp.where(allowed, jnp.exp(masked - m_new), 0.0)
            factor = jnp.exp(m_old - m_new)
            l_sc[g] = l_sc[g] * factor + jnp.sum(weights, axis=1, keepdims=True)
            update = jnp.dot(weights.astype(jnp.bfloat16), v_ref[g], preferred_element_type=jnp.float32)
            acc_sc[g] = acc_sc[g] * factor + update
            m_sc[g] = m_new

    @pl.when(ki == pl.num_programs(1) - 1)
    def _():
        o_ref[...] = (acc_sc[...] / l_sc[...]).astype(o_ref.dtype)


def attend(queries, keyvals_all, seg_ids, live, first_row):
    group_rows, groups = queries.shape[:2]
    tokens = keyvals_all.shape[0]
    tq = min(TQ, group_rows)
    nq = group_rows // tq
    bk = min(BK, tokens)
    nk = tokens // bk
    rows = QPK * tq
    q = queries.reshape(nq, tq, groups, QPK, HD).transpose(0, 2, 3, 1, 4).reshape(nq, groups, rows, HD)
    k = keyvals_all[:, :, :HD].transpose(1, 0, 2)
    v = keyvals_all[:, :, HD:].transpose(1, 0, 2)
    tok = first_row + jnp.arange(group_rows, dtype=jnp.int32)
    seg_here = lax.dynamic_slice_in_dim(seg_ids, first_row, group_rows, 0)

    def column(x):
        return jnp.broadcast_to(x.reshape(nq, 1, tq), (nq, QPK, tq)).reshape(nq, rows, 1)

    qidx = column(tok)
    qseg = column(seg_here)
    kseg = seg_ids.reshape(1, tokens)
    klive = live.reshape(1, tokens)
    base = jnp.reshape(first_row, (1,)).astype(jnp.int32)

    def kmap(qi, ki, seg_sm, base_sm):
        return jnp.minimum(ki, (base_sm[0] + qi * tq + tq - 1) // bk)

    grid_spec = pltpu.PrefetchScalarGridSpec(
        num_scalar_prefetch=2,
        grid=(nq, nk),
        in_specs=[
            pl.BlockSpec((None, groups, rows, HD), lambda qi, ki, s, b: (qi, 0, 0, 0)),
            pl.BlockSpec((groups, bk, HD), lambda qi, ki, s, b: (0, kmap(qi, ki, s, b), 0)),
            pl.BlockSpec((groups, bk, HD), lambda qi, ki, s, b: (0, kmap(qi, ki, s, b), 0)),
            pl.BlockSpec((None, rows, 1), lambda qi, ki, s, b: (qi, 0, 0)),
            pl.BlockSpec((None, rows, 1), lambda qi, ki, s, b: (qi, 0, 0)),
            pl.BlockSpec((1, bk), lambda qi, ki, s, b: (0, kmap(qi, ki, s, b))),
            pl.BlockSpec((1, bk), lambda qi, ki, s, b: (0, kmap(qi, ki, s, b))),
        ],
        out_specs=pl.BlockSpec((None, groups, rows, HD), lambda qi, ki, s, b: (qi, 0, 0, 0)),
        scratch_shapes=[
            pltpu.VMEM((groups, rows, 1), jnp.float32),
            pltpu.VMEM((groups, rows, 1), jnp.float32),
            pltpu.VMEM((groups, rows, HD), jnp.float32),
        ],
    )
    out = pl.pallas_call(
        attention_kernel,
        out_shape=jax.ShapeDtypeStruct((nq, groups, rows, HD), jnp.bfloat16),
        grid_spec=grid_spec,
        compiler_params=pltpu.CompilerParams(dimension_semantics=("arbitrary", "arbitrary")),
        interpret=INTERPRET,
    )(seg_ids, base, q, k, v, qseg, qidx, kseg, klive)
    out = out.reshape(nq, groups, QPK, tq, HD).transpose(0, 3, 1, 2, 4)
    return out.reshape(group_rows, groups * QPK * HD)


def shards(hidden, w_qkv, w_out, seg_ids, live, page_table):
    heads_n = lax.axis_size("head")
    seq_at = lax.axis_index("seq")
    groups_here = KVH // heads_n
    per_group = (QPK + 2) * HD
    columns = groups_here * per_group
    local = jnp.dot(hidden, w_qkv, preferred_element_type=jnp.float32).astype(jnp.bfloat16)
    local = local.reshape(local.shape[0], heads_n, columns)
    grouped = lax.all_to_all(local, "head", split_axis=1, concat_axis=0, tiled=True)
    group_rows = grouped.shape[0]
    shaped = grouped.reshape(group_rows, groups_here, QPK + 2, HD)
    queries = shaped[:, :, :QPK]
    keyvals = shaped[:, :, QPK:].reshape(group_rows, groups_here, 2 * HD)
    first_row = (seq_at * group_rows).astype(jnp.int32)
    piece = lax.all_gather(keyvals, "seq", axis=0, tiled=True)
    attended = attend(queries, piece, seg_ids, live, first_row)
    own_tokens = lax.all_to_all(attended, "head", split_axis=0, concat_axis=1, tiled=True)
    mixed = jnp.dot(own_tokens, w_out, preferred_element_type=jnp.float32).astype(jnp.bfloat16)
    pages_n = page_table.shape[0]
    page_count = pages_n // lax.axis_size("seq")
    all_pages = piece.reshape(pages_n, PAGE, groups_here, 2 * HD)
    wanted = seq_at * page_count + jnp.arange(page_count, dtype=jnp.int32)
    hits = page_table[None, :] == wanted[:, None]
    logical = jnp.sum(jnp.where(hits, jnp.arange(pages_n, dtype=jnp.int32)[None, :], 0), axis=1)
    kv_pool = jnp.take(all_pages, logical, axis=0).transpose(2, 0, 1, 3)
    return (mixed, kv_pool)


def solution(mesh):
    placed = (P(("seq", "head"), None), P(), P(), P(), P(), P())
    return jax.shard_map(
        shards,
        mesh=mesh,
        in_specs=placed,
        out_specs=(P(("seq", "head"), None), P("head", "seq", None, None)),
        check_vma=False,
    )
```

```python
import functools

import jax
import jax.numpy as jnp
from jax import lax
from jax.experimental import pallas as pl
from jax.experimental.pallas import tpu as pltpu
from jax.sharding import PartitionSpec as P

KVH = 8
HD = 64
PAGE = 16
QPK = 4
TQ = 256
BK = 512
INTERPRET = False


def attention_kernel(seg_sm, base_sm, q_ref, kv_ref, qseg_ref, qidx_ref, kseg_ref, klive_ref,
                     o_ref, m_sc, l_sc, acc_sc):
    qi = pl.program_id(0)
    ki = pl.program_id(1)
    groups = q_ref.shape[0]
    tq = q_ref.shape[1] // QPK
    bk = kv_ref.shape[1]

    @pl.when(ki == 0)
    def _():
        m_sc[...] = jnp.full(m_sc.shape, -1e30, jnp.float32)
        l_sc[...] = jnp.zeros(l_sc.shape, jnp.float32)
        acc_sc[...] = jnp.zeros(acc_sc.shape, jnp.float32)

    q_first = base_sm[0] + qi * tq
    q_last = q_first + tq - 1
    k_first = ki * bk
    k_last = k_first + bk - 1
    active = (k_first <= q_last) & (seg_sm[k_first] <= seg_sm[q_last]) & (seg_sm[k_last] >= seg_sm[q_first])

    @pl.when(active)
    def _():
        kidx = k_first + lax.broadcasted_iota(jnp.int32, (1, bk), 1)
        qidx = qidx_ref[...]
        allowed = (kseg_ref[...] == qseg_ref[...]) & (kidx <= qidx)
        allowed = allowed & ((klive_ref[...] == 1) | (kidx == qidx))
        for g in range(groups):
            scores = lax.dot_general(
                q_ref[g], kv_ref[g], (((1,), (1,)), ((), ())), preferred_element_type=jnp.float32
            ) * 0.015625
            masked = jnp.where(allowed, scores, -1e30)
            m_old = m_sc[g]
            m_new = jnp.maximum(m_old, jnp.max(masked, axis=1, keepdims=True))
            weights = jnp.where(allowed, jnp.exp(masked - m_new), 0.0)
            factor = jnp.exp(m_old - m_new)
            l_sc[g] = l_sc[g] * factor + jnp.sum(weights, axis=1, keepdims=True)
            update = jnp.dot(weights.astype(jnp.bfloat16), kv_ref[g], preferred_element_type=jnp.float32)
            acc_sc[g] = acc_sc[g] * factor + update
            m_sc[g] = m_new

    @pl.when(ki == pl.num_programs(1) - 1)
    def _():
        for g in range(groups):
            for c in range(QPK):
                lo = (g * QPK + c) * HD
                part = acc_sc[g, c * tq:(c + 1) * tq, HD:] / l_sc[g, c * tq:(c + 1) * tq]
                o_ref[:, lo:lo + HD] = part.astype(o_ref.dtype)


def attend(queries, keyvals_all, seg_ids, live, first_row):
    group_rows, groups = queries.shape[:2]
    tokens = keyvals_all.shape[1]
    tq = min(TQ, group_rows)
    nq = group_rows // tq
    bk = min(BK, tokens)
    nk = tokens // bk
    rows = QPK * tq
    q = queries.reshape(nq, tq, groups, QPK, HD).transpose(0, 2, 3, 1, 4).reshape(nq, groups, rows, HD)
    q = jnp.concatenate([q, jnp.zeros_like(q)], axis=-1)
    tok = first_row + jnp.arange(group_rows, dtype=jnp.int32)
    seg_here = lax.dynamic_slice_in_dim(seg_ids, first_row, group_rows, 0)

    def column(x):
        return jnp.broadcast_to(x.reshape(nq, 1, tq), (nq, QPK, tq)).reshape(nq, rows, 1)

    qidx = column(tok)
    qseg = column(seg_here)
    kseg = seg_ids.reshape(1, tokens)
    klive = live.reshape(1, tokens)
    base = jnp.reshape(first_row, (1,)).astype(jnp.int32)

    def kmap(qi, ki, seg_sm, base_sm):
        return jnp.minimum(ki, (base_sm[0] + qi * tq + tq - 1) // bk)

    grid_spec = pltpu.PrefetchScalarGridSpec(
        num_scalar_prefetch=2,
        grid=(nq, nk),
        in_specs=[
            pl.BlockSpec((None, groups, rows, 2 * HD), lambda qi, ki, s, b: (qi, 0, 0, 0)),
            pl.BlockSpec((groups, bk, 2 * HD), lambda qi, ki, s, b: (0, kmap(qi, ki, s, b), 0)),
            pl.BlockSpec((None, rows, 1), lambda qi, ki, s, b: (qi, 0, 0)),
            pl.BlockSpec((None, rows, 1), lambda qi, ki, s, b: (qi, 0, 0)),
            pl.BlockSpec((1, bk), lambda qi, ki, s, b: (0, kmap(qi, ki, s, b))),
            pl.BlockSpec((1, bk), lambda qi, ki, s, b: (0, kmap(qi, ki, s, b))),
        ],
        out_specs=pl.BlockSpec((tq, groups * QPK * HD), lambda qi, ki, s, b: (qi, 0)),
        scratch_shapes=[
            pltpu.VMEM((groups, rows, 1), jnp.float32),
            pltpu.VMEM((groups, rows, 1), jnp.float32),
            pltpu.VMEM((groups, rows, 2 * HD), jnp.float32),
        ],
    )
    return pl.pallas_call(
        attention_kernel,
        out_shape=jax.ShapeDtypeStruct((group_rows, groups * QPK * HD), jnp.bfloat16),
        grid_spec=grid_spec,
        compiler_params=pltpu.CompilerParams(dimension_semantics=("arbitrary", "arbitrary")),
        interpret=INTERPRET,
    )(seg_ids, base, q, keyvals_all, qseg, qidx, kseg, klive)


def shards(hidden, w_qkv, w_out, seg_ids, live, page_table):
    heads_n = lax.axis_size("head")
    seq_at = lax.axis_index("seq")
    groups_here = KVH // heads_n
    per_group = (QPK + 2) * HD
    columns = groups_here * per_group
    local = jnp.dot(hidden, w_qkv, preferred_element_type=jnp.float32).astype(jnp.bfloat16)
    local = local.reshape(local.shape[0], heads_n, columns)
    grouped = lax.all_to_all(local, "head", split_axis=1, concat_axis=0, tiled=True)
    group_rows = grouped.shape[0]
    shaped = grouped.reshape(group_rows, groups_here, QPK + 2, HD)
    queries = shaped[:, :, :QPK]
    keyvals = shaped[:, :, QPK:].reshape(group_rows, groups_here, 2 * HD).transpose(1, 0, 2)
    first_row = (seq_at * group_rows).astype(jnp.int32)
    piece = lax.all_gather(keyvals, "seq", axis=1, tiled=True)
    attended = attend(queries, piece, seg_ids, live, first_row)
    own_tokens = lax.all_to_all(attended, "head", split_axis=0, concat_axis=1, tiled=True)
    mixed = jnp.dot(own_tokens, w_out, preferred_element_type=jnp.float32).astype(jnp.bfloat16)
    pages_n = page_table.shape[0]
    page_count = pages_n // lax.axis_size("seq")
    all_pages = piece.reshape(groups_here, pages_n, PAGE, 2 * HD)
    wanted = seq_at * page_count + jnp.arange(page_count, dtype=jnp.int32)
    hits = page_table[None, :] == wanted[:, None]
    logical = jnp.sum(jnp.where(hits, jnp.arange(pages_n, dtype=jnp.int32)[None, :], 0), axis=1)
    kv_pool = jnp.take(all_pages, logical, axis=1)
    return (mixed, kv_pool)


def solution(mesh):
    placed = (P(("seq", "head"), None), P(), P(), P(), P(), P())
    return jax.shard_map(
        shards,
        mesh=mesh,
        in_specs=placed,
        out_specs=(P(("seq", "head"), None), P("head", "seq", None, None)),
        check_vma=False,
    )
```

```python
import functools

import jax
import jax.numpy as jnp
from jax import lax
from jax.experimental import pallas as pl
from jax.experimental.pallas import tpu as pltpu
from jax.sharding import PartitionSpec as P

KVH = 8
HD = 64
PAGE = 16
QPK = 4
TQ = 256
BK = 512
INTERPRET = False


def attention_kernel(seg_sm, base_sm, q_ref, kv_ref, qseg_ref, qidx_ref, kseg_ref, klive_ref,
                     o_ref, m_sc, l_sc, acc_sc):
    qi = pl.program_id(0)
    ki = pl.program_id(1)
    groups = q_ref.shape[0]
    tq = q_ref.shape[1] // QPK
    bk = kv_ref.shape[1]

    @pl.when(ki == 0)
    def _():
        m_sc[...] = jnp.full(m_sc.shape, -1e30, jnp.float32)
        l_sc[...] = jnp.zeros(l_sc.shape, jnp.float32)
        acc_sc[...] = jnp.zeros(acc_sc.shape, jnp.float32)

    q_first = base_sm[0] + qi * tq
    q_last = q_first + tq - 1
    k_first = ki * bk
    k_last = k_first + bk - 1
    active = (k_first <= q_last) & (seg_sm[k_first] <= seg_sm[q_last]) & (seg_sm[k_last] >= seg_sm[q_first])

    @pl.when(active)
    def _():
        kidx = k_first + lax.broadcasted_iota(jnp.int32, (1, bk), 1)
        qidx = qidx_ref[...]
        allowed = (kseg_ref[...] == qseg_ref[...]) & (kidx <= qidx)
        allowed = allowed & ((klive_ref[...] == 1) | (kidx == qidx))
        for g in range(groups):
            scores = lax.dot_general(
                q_ref[g], kv_ref[g], (((1,), (1,)), ((), ())), preferred_element_type=jnp.float32
            ) * 0.015625
            masked = jnp.where(allowed, scores, -1e30)
            m_old = m_sc[g]
            m_new = jnp.maximum(m_old, jnp.max(masked, axis=1, keepdims=True))
            weights = jnp.where(allowed, jnp.exp(masked - m_new), 0.0)
            factor = jnp.exp(m_old - m_new)
            l_sc[g] = l_sc[g] * factor + jnp.sum(weights, axis=1, keepdims=True)
            update = jnp.dot(weights.astype(jnp.bfloat16), kv_ref[g], preferred_element_type=jnp.float32)
            acc_sc[g] = acc_sc[g] * factor + update
            m_sc[g] = m_new

    @pl.when(ki == pl.num_programs(1) - 1)
    def _():
        for g in range(groups):
            for c in range(QPK):
                lo = (g * QPK + c) * HD
                part = acc_sc[g, c * tq:(c + 1) * tq, HD:] / l_sc[g, c * tq:(c + 1) * tq]
                o_ref[:, lo:lo + HD] = part.astype(o_ref.dtype)


def attend(queries, keyvals_all, seg_ids, live, first_row):
    group_rows, groups = queries.shape[:2]
    tokens = keyvals_all.shape[1]
    tq = min(TQ, group_rows)
    nq = group_rows // tq
    bk = min(BK, tokens)
    nk = tokens // bk
    rows = QPK * tq
    q = queries.reshape(nq, tq, groups, QPK, HD).transpose(0, 2, 3, 1, 4).reshape(nq, groups, rows, HD)
    q = jnp.concatenate([q, jnp.zeros_like(q)], axis=-1)
    tok = first_row + jnp.arange(group_rows, dtype=jnp.int32)
    seg_here = lax.dynamic_slice_in_dim(seg_ids, first_row, group_rows, 0)

    def column(x):
        return jnp.broadcast_to(x.reshape(nq, 1, tq), (nq, QPK, tq)).reshape(nq, rows, 1)

    qidx = column(tok)
    qseg = column(seg_here)
    kseg = seg_ids.reshape(1, tokens)
    klive = live.reshape(1, tokens)
    base = jnp.reshape(first_row, (1,)).astype(jnp.int32)

    def kmap(qi, ki, seg_sm, base_sm):
        return jnp.minimum(ki, (base_sm[0] + qi * tq + tq - 1) // bk)

    grid_spec = pltpu.PrefetchScalarGridSpec(
        num_scalar_prefetch=2,
        grid=(nq, nk),
        in_specs=[
            pl.BlockSpec((None, groups, rows, 2 * HD), lambda qi, ki, s, b: (qi, 0, 0, 0)),
            pl.BlockSpec((groups, bk, 2 * HD), lambda qi, ki, s, b: (0, kmap(qi, ki, s, b), 0)),
            pl.BlockSpec((None, rows, 1), lambda qi, ki, s, b: (qi, 0, 0)),
            pl.BlockSpec((None, rows, 1), lambda qi, ki, s, b: (qi, 0, 0)),
            pl.BlockSpec((1, bk), lambda qi, ki, s, b: (0, kmap(qi, ki, s, b))),
            pl.BlockSpec((1, bk), lambda qi, ki, s, b: (0, kmap(qi, ki, s, b))),
        ],
        out_specs=pl.BlockSpec((tq, groups * QPK * HD), lambda qi, ki, s, b: (qi, 0)),
        scratch_shapes=[
            pltpu.VMEM((groups, rows, 1), jnp.float32),
            pltpu.VMEM((groups, rows, 1), jnp.float32),
            pltpu.VMEM((groups, rows, 2 * HD), jnp.float32),
        ],
    )
    return pl.pallas_call(
        attention_kernel,
        out_shape=jax.ShapeDtypeStruct((group_rows, groups * QPK * HD), jnp.bfloat16),
        grid_spec=grid_spec,
        compiler_params=pltpu.CompilerParams(dimension_semantics=("arbitrary", "arbitrary")),
        interpret=INTERPRET,
    )(seg_ids, base, q, keyvals_all, qseg, qidx, kseg, klive)


def shards(hidden, w_qkv, w_out, seg_ids, live, page_table):
    heads_n = lax.axis_size("head")
    seq_at = lax.axis_index("seq")
    groups_here = KVH // heads_n
    per_group = (QPK + 2) * HD
    columns = groups_here * per_group
    local = jnp.dot(hidden, w_qkv, preferred_element_type=jnp.float32).astype(jnp.bfloat16)
    own_rows = local.shape[0]
    local = local.reshape(own_rows, heads_n, groups_here, QPK + 2, HD)
    kv_local = local[:, :, :, QPK:].reshape(own_rows, heads_n, groups_here * 2 * HD)
    kv_group = lax.all_to_all(kv_local, "head", split_axis=1, concat_axis=0, tiled=True)
    group_rows = kv_group.shape[0]
    keyvals = kv_group.reshape(group_rows, groups_here, 2 * HD).transpose(1, 0, 2)
    piece = lax.all_gather(keyvals, "seq", axis=1, tiled=True)
    q_local = local[:, :, :, :QPK].reshape(own_rows, heads_n, groups_here * QPK * HD)
    q_group = lax.all_to_all(q_local, "head", split_axis=1, concat_axis=0, tiled=True)
    queries = q_group.reshape(group_rows, groups_here, QPK, HD)
    first_row = (seq_at * group_rows).astype(jnp.int32)
    attended = attend(queries, piece, seg_ids, live, first_row)
    own_tokens = lax.all_to_all(attended, "head", split_axis=0, concat_axis=1, tiled=True)
    mixed = jnp.dot(own_tokens, w_out, preferred_element_type=jnp.float32).astype(jnp.bfloat16)
    pages_n = page_table.shape[0]
    page_count = pages_n // lax.axis_size("seq")
    all_pages = piece.reshape(groups_here, pages_n, PAGE, 2 * HD)
    wanted = seq_at * page_count + jnp.arange(page_count, dtype=jnp.int32)
    hits = page_table[None, :] == wanted[:, None]
    logical = jnp.sum(jnp.where(hits, jnp.arange(pages_n, dtype=jnp.int32)[None, :], 0), axis=1)
    kv_pool = jnp.take(all_pages, logical, axis=1)
    return (mixed, kv_pool)


def solution(mesh):
    placed = (P(("seq", "head"), None), P(), P(), P(), P(), P())
    return jax.shard_map(
        shards,
        mesh=mesh,
        in_specs=placed,
        out_specs=(P(("seq", "head"), None), P("head", "seq", None, None)),
        check_vma=False,
    )
```

```python
import functools

import jax
import jax.numpy as jnp
from jax import lax
from jax.experimental import pallas as pl
from jax.experimental.pallas import tpu as pltpu
from jax.sharding import PartitionSpec as P

KVH = 8
HD = 64
PAGE = 16
QPK = 4
TQ = 256
BK = 512
INTERPRET = False


def attention_kernel(seg_sm, bounds_sm, q_ref, kv_ref, qseg_ref, qidx_ref, kseg_ref, klive_ref,
                     o_ref, m_sc, l_sc, acc_sc):
    qi = pl.program_id(0)
    ki = pl.program_id(1)
    groups = q_ref.shape[0]
    tq = q_ref.shape[1] // QPK
    bk = kv_ref.shape[1]

    @pl.when(ki == 0)
    def _():
        m_sc[...] = jnp.full(m_sc.shape, -1e30, jnp.float32)
        l_sc[...] = jnp.zeros(l_sc.shape, jnp.float32)
        acc_sc[...] = jnp.zeros(acc_sc.shape, jnp.float32)

    q_first = bounds_sm[2 * qi]
    q_last = bounds_sm[2 * qi + 1]
    k_first = ki * bk
    k_last = k_first + bk - 1
    active = (k_first <= q_last) & (seg_sm[k_first] <= seg_sm[q_last]) & (seg_sm[k_last] >= seg_sm[q_first])

    @pl.when(active)
    def _():
        kidx = k_first + lax.broadcasted_iota(jnp.int32, (1, bk), 1)
        qidx = qidx_ref[...]
        allowed = (kseg_ref[...] == qseg_ref[...]) & (kidx <= qidx)
        allowed = allowed & ((klive_ref[...] == 1) | (kidx == qidx))
        for g in range(groups):
            scores = lax.dot_general(
                q_ref[g], kv_ref[g], (((1,), (1,)), ((), ())), preferred_element_type=jnp.float32
            ) * 0.015625
            masked = jnp.where(allowed, scores, -1e30)
            m_old = m_sc[g]
            m_new = jnp.maximum(m_old, jnp.max(masked, axis=1, keepdims=True))
            weights = jnp.where(allowed, jnp.exp(masked - m_new), 0.0)
            factor = jnp.exp(m_old - m_new)
            l_sc[g] = l_sc[g] * factor + jnp.sum(weights, axis=1, keepdims=True)
            update = jnp.dot(weights.astype(jnp.bfloat16), kv_ref[g], preferred_element_type=jnp.float32)
            acc_sc[g] = acc_sc[g] * factor + update
            m_sc[g] = m_new

    @pl.when(ki == pl.num_programs(1) - 1)
    def _():
        for g in range(groups):
            for c in range(QPK):
                lo = (g * QPK + c) * HD
                part = acc_sc[g, c * tq:(c + 1) * tq, HD:] / l_sc[g, c * tq:(c + 1) * tq]
                o_ref[:, lo:lo + HD] = part.astype(o_ref.dtype)


def attend(queries, keyvals_all, seg_ids, live, tok):
    group_rows, groups = queries.shape[:2]
    tokens = keyvals_all.shape[1]
    tq = min(TQ, group_rows)
    nq = group_rows // tq
    bk = min(BK, tokens)
    nk = tokens // bk
    rows = QPK * tq
    q = queries.reshape(nq, tq, groups, QPK, HD).transpose(0, 2, 3, 1, 4).reshape(nq, groups, rows, HD)
    q = jnp.concatenate([q, jnp.zeros_like(q)], axis=-1)
    tiles = tok.reshape(nq, tq)
    bounds = jnp.stack([jnp.min(tiles, axis=1), jnp.max(tiles, axis=1)], axis=1).reshape(2 * nq)

    def column(x):
        return jnp.broadcast_to(x.reshape(nq, 1, tq), (nq, QPK, tq)).reshape(nq, rows, 1)

    qidx = column(tok)
    qseg = column(jnp.take(seg_ids, tok))
    kseg = seg_ids.reshape(1, tokens)
    klive = live.reshape(1, tokens)

    def kmap(qi, ki, seg_sm, bounds_sm):
        return jnp.minimum(ki, bounds_sm[2 * qi + 1] // bk)

    grid_spec = pltpu.PrefetchScalarGridSpec(
        num_scalar_prefetch=2,
        grid=(nq, nk),
        in_specs=[
            pl.BlockSpec((None, groups, rows, 2 * HD), lambda qi, ki, s, b: (qi, 0, 0, 0)),
            pl.BlockSpec((groups, bk, 2 * HD), lambda qi, ki, s, b: (0, kmap(qi, ki, s, b), 0)),
            pl.BlockSpec((None, rows, 1), lambda qi, ki, s, b: (qi, 0, 0)),
            pl.BlockSpec((None, rows, 1), lambda qi, ki, s, b: (qi, 0, 0)),
            pl.BlockSpec((1, bk), lambda qi, ki, s, b: (0, kmap(qi, ki, s, b))),
            pl.BlockSpec((1, bk), lambda qi, ki, s, b: (0, kmap(qi, ki, s, b))),
        ],
        out_specs=pl.BlockSpec((tq, groups * QPK * HD), lambda qi, ki, s, b: (qi, 0)),
        scratch_shapes=[
            pltpu.VMEM((groups, rows, 1), jnp.float32),
            pltpu.VMEM((groups, rows, 1), jnp.float32),
            pltpu.VMEM((groups, rows, 2 * HD), jnp.float32),
        ],
    )
    return pl.pallas_call(
        attention_kernel,
        out_shape=jax.ShapeDtypeStruct((group_rows, groups * QPK * HD), jnp.bfloat16),
        grid_spec=grid_spec,
        compiler_params=pltpu.CompilerParams(dimension_semantics=("arbitrary", "arbitrary")),
        interpret=INTERPRET,
    )(seg_ids, bounds, q, keyvals_all, qseg, qidx, kseg, klive)


def shards(hidden, w_qkv, w_out, seg_ids, live, page_table):
    heads_n = lax.axis_size("head")
    seq_at = lax.axis_index("seq")
    groups_here = KVH // heads_n
    per_group = (QPK + 2) * HD
    columns = groups_here * per_group
    local = jnp.dot(hidden, w_qkv, preferred_element_type=jnp.float32).astype(jnp.bfloat16)
    own_rows = local.shape[0]
    local = local.reshape(own_rows, heads_n, groups_here, QPK + 2, HD)
    kv_local = local[:, :, :, QPK:].reshape(own_rows, heads_n, groups_here * 2 * HD)
    kv_group = lax.all_to_all(kv_local, "head", split_axis=1, concat_axis=0, tiled=True)
    group_rows = kv_group.shape[0]
    keyvals = kv_group.reshape(group_rows, groups_here, 2 * HD).transpose(1, 0, 2)
    piece = lax.all_gather(keyvals, "seq", axis=1, tiled=True)
    q_local = local[:, :, :, :QPK].reshape(own_rows, heads_n, groups_here * QPK * HD)
    q_group = lax.all_to_all(q_local, "head", split_axis=1, concat_axis=0, tiled=True)
    queries = q_group.reshape(group_rows, groups_here, QPK, HD)
    first_row = (seq_at * group_rows).astype(jnp.int32)
    own_rows = group_rows // heads_n
    halves = 2 if own_rows % 16 == 0 else 1
    part = own_rows // halves
    by_dest = queries.reshape(heads_n, halves, part, groups_here, QPK, HD)
    tok_grid = first_row + jnp.arange(group_rows, dtype=jnp.int32).reshape(heads_n, halves, part)
    mixed_parts = []
    for j in range(halves):
        q_half = by_dest[:, j].reshape(heads_n * part, groups_here, QPK, HD)
        tok = tok_grid[:, j].reshape(heads_n * part)
        attended = attend(q_half, piece, seg_ids, live, tok)
        own = lax.all_to_all(attended, "head", split_axis=0, concat_axis=1, tiled=True)
        mixed_parts.append(jnp.dot(own, w_out, preferred_element_type=jnp.float32).astype(jnp.bfloat16))
    mixed = jnp.concatenate(mixed_parts, axis=0)
    pages_n = page_table.shape[0]
    page_count = pages_n // lax.axis_size("seq")
    all_pages = piece.reshape(groups_here, pages_n, PAGE, 2 * HD)
    wanted = seq_at * page_count + jnp.arange(page_count, dtype=jnp.int32)
    hits = page_table[None, :] == wanted[:, None]
    logical = jnp.sum(jnp.where(hits, jnp.arange(pages_n, dtype=jnp.int32)[None, :], 0), axis=1)
    kv_pool = jnp.take(all_pages, logical, axis=1)
    return (mixed, kv_pool)


def solution(mesh):
    placed = (P(("seq", "head"), None), P(), P(), P(), P(), P())
    return jax.shard_map(
        shards,
        mesh=mesh,
        in_specs=placed,
        out_specs=(P(("seq", "head"), None), P("head", "seq", None, None)),
        check_vma=False,
    )
```

```python
import functools

import jax
import jax.numpy as jnp
from jax import lax
from jax.experimental import pallas as pl
from jax.experimental.pallas import tpu as pltpu
from jax.sharding import PartitionSpec as P

KVH = 8
HD = 64
PAGE = 16
QPK = 4
TQ = 256
BK = 512
INTERPRET = False


def attention_kernel(seg_sm, base_sm, q_ref, kv_ref, qseg_ref, qidx_ref, kseg_ref, klive_ref,
                     o_ref, m_sc, l_sc, acc_sc):
    qi = pl.program_id(0)
    ki = pl.program_id(1)
    groups = q_ref.shape[0]
    tq = q_ref.shape[1] // QPK
    bk = kv_ref.shape[1]

    @pl.when(ki == 0)
    def _():
        m_sc[...] = jnp.full(m_sc.shape, -1e30, jnp.float32)
        l_sc[...] = jnp.zeros(l_sc.shape, jnp.float32)
        acc_sc[...] = jnp.zeros(acc_sc.shape, jnp.float32)

    q_first = base_sm[0] + qi * tq
    q_last = q_first + tq - 1
    k_first = ki * bk
    k_last = k_first + bk - 1
    active = (k_first <= q_last) & (seg_sm[k_first] <= seg_sm[q_last]) & (seg_sm[k_last] >= seg_sm[q_first])

    @pl.when(active)
    def _():
        kidx = k_first + lax.broadcasted_iota(jnp.int32, (1, bk), 1)
        qidx = qidx_ref[...]
        allowed = (kseg_ref[...] == qseg_ref[...]) & (kidx <= qidx)
        allowed = allowed & ((klive_ref[...] == 1) | (kidx == qidx))
        for g in range(groups):
            scores = lax.dot_general(
                q_ref[g], kv_ref[g], (((1,), (1,)), ((), ())), preferred_element_type=jnp.float32
            ) * 0.015625
            masked = jnp.where(allowed, scores, -1e30)
            m_old = m_sc[g]
            m_new = jnp.maximum(m_old, jnp.max(masked, axis=1, keepdims=True))
            weights = jnp.where(allowed, jnp.exp(masked - m_new), 0.0)
            factor = jnp.exp(m_old - m_new)
            l_sc[g] = l_sc[g] * factor + jnp.sum(weights, axis=1, keepdims=True)
            update = jnp.dot(weights.astype(jnp.bfloat16), kv_ref[g], preferred_element_type=jnp.float32)
            acc_sc[g] = acc_sc[g] * factor + update
            m_sc[g] = m_new

    @pl.when(ki == pl.num_programs(1) - 1)
    def _():
        for g in range(groups):
            for c in range(QPK):
                lo = (g * QPK + c) * HD
                part = acc_sc[g, c * tq:(c + 1) * tq, HD:] / l_sc[g, c * tq:(c + 1) * tq]
                o_ref[:, lo:lo + HD] = part.astype(o_ref.dtype)


def attend(queries, keyvals_all, seg_ids, live, first_row):
    group_rows, groups = queries.shape[:2]
    tokens = keyvals_all.shape[1]
    tq = min(TQ, group_rows)
    nq = group_rows // tq
    bk = min(BK, tokens)
    nk = tokens // bk
    rows = QPK * tq
    q = queries.reshape(nq, tq, groups, QPK, HD).transpose(0, 2, 3, 1, 4).reshape(nq, groups, rows, HD)
    q = jnp.concatenate([q, jnp.zeros_like(q)], axis=-1)
    tok = first_row + jnp.arange(group_rows, dtype=jnp.int32)
    seg_here = lax.dynamic_slice_in_dim(seg_ids, first_row, group_rows, 0)

    def column(x):
        return jnp.broadcast_to(x.reshape(nq, 1, tq), (nq, QPK, tq)).reshape(nq, rows, 1)

    qidx = column(tok)
    qseg = column(seg_here)
    kseg = seg_ids.reshape(1, tokens)
    klive = live.reshape(1, tokens)
    base = jnp.reshape(first_row, (1,)).astype(jnp.int32)

    def kmap(qi, ki, seg_sm, base_sm):
        return jnp.minimum(ki, (base_sm[0] + qi * tq + tq - 1) // bk)

    grid_spec = pltpu.PrefetchScalarGridSpec(
        num_scalar_prefetch=2,
        grid=(nq, nk),
        in_specs=[
            pl.BlockSpec((None, groups, rows, 2 * HD), lambda qi, ki, s, b: (qi, 0, 0, 0)),
            pl.BlockSpec((groups, bk, 2 * HD), lambda qi, ki, s, b: (0, kmap(qi, ki, s, b), 0)),
            pl.BlockSpec((None, rows, 1), lambda qi, ki, s, b: (qi, 0, 0)),
            pl.BlockSpec((None, rows, 1), lambda qi, ki, s, b: (qi, 0, 0)),
            pl.BlockSpec((1, bk), lambda qi, ki, s, b: (0, kmap(qi, ki, s, b))),
            pl.BlockSpec((1, bk), lambda qi, ki, s, b: (0, kmap(qi, ki, s, b))),
        ],
        out_specs=pl.BlockSpec((tq, groups * QPK * HD), lambda qi, ki, s, b: (qi, 0)),
        scratch_shapes=[
            pltpu.VMEM((groups, rows, 1), jnp.float32),
            pltpu.VMEM((groups, rows, 1), jnp.float32),
            pltpu.VMEM((groups, rows, 2 * HD), jnp.float32),
        ],
    )
    return pl.pallas_call(
        attention_kernel,
        out_shape=jax.ShapeDtypeStruct((group_rows, groups * QPK * HD), jnp.bfloat16),
        grid_spec=grid_spec,
        compiler_params=pltpu.CompilerParams(dimension_semantics=("arbitrary", "arbitrary")),
        interpret=INTERPRET,
    )(seg_ids, base, q, keyvals_all, qseg, qidx, kseg, klive)


def exchange(chunks, heads_n, head_at):
    got = [lax.dynamic_index_in_dim(chunks, head_at, 0, keepdims=False)]
    for d in range(1, heads_n):
        mine = lax.dynamic_index_in_dim(chunks, (head_at + d) % heads_n, 0, keepdims=False)
        pairs = [(i, (i + d) % heads_n) for i in range(heads_n)]
        got.append(lax.ppermute(mine, "head", pairs))
    return got


def shards(hidden, w_qkv, w_out, seg_ids, live, page_table):
    heads_n = lax.axis_size("head")
    head_at = lax.axis_index("head")
    seq_at = lax.axis_index("seq")
    groups_here = KVH // heads_n
    per_group = (QPK + 2) * HD
    columns = groups_here * per_group
    local = jnp.dot(hidden, w_qkv, preferred_element_type=jnp.float32).astype(jnp.bfloat16)
    own_rows = local.shape[0]
    local = local.reshape(own_rows, heads_n, groups_here, QPK + 2, HD)
    kv_local = local[:, :, :, QPK:].reshape(own_rows, heads_n, groups_here, 2 * HD).transpose(1, 2, 0, 3)
    kv_got = exchange(kv_local, heads_n, head_at)
    kv_by_shift = jnp.stack(kv_got, axis=0)
    shift_of = (head_at - jnp.arange(heads_n, dtype=jnp.int32)) % heads_n
    kv_by_src = jnp.take(kv_by_shift, shift_of, axis=0)
    group_rows = own_rows * heads_n
    keyvals = kv_by_src.transpose(1, 0, 2, 3).reshape(groups_here, group_rows, 2 * HD)
    piece = lax.all_gather(keyvals, "seq", axis=1, tiled=True)
    q_local = local[:, :, :, :QPK].reshape(own_rows, heads_n, groups_here * QPK * HD)
    q_group = lax.all_to_all(q_local, "head", split_axis=1, concat_axis=0, tiled=True)
    queries = q_group.reshape(group_rows, groups_here, QPK, HD)
    first_row = (seq_at * group_rows).astype(jnp.int32)
    attended = attend(queries, piece, seg_ids, live, first_row)
    width = attended.shape[1]
    att_got = exchange(attended.reshape(heads_n, own_rows, width), heads_n, head_at)
    total = None
    for d in range(heads_n):
        src_head = (head_at - d) % heads_n
        w_rows = lax.dynamic_slice_in_dim(w_out, src_head * width, width, 0)
        partial = jnp.dot(att_got[d], w_rows, preferred_element_type=jnp.float32)
        total = partial if total is None else total + partial
    mixed = total.astype(jnp.bfloat16)
    pages_n = page_table.shape[0]
    page_count = pages_n // lax.axis_size("seq")
    all_pages = piece.reshape(groups_here, pages_n, PAGE, 2 * HD)
    wanted = seq_at * page_count + jnp.arange(page_count, dtype=jnp.int32)
    hits = page_table[None, :] == wanted[:, None]
    logical = jnp.sum(jnp.where(hits, jnp.arange(pages_n, dtype=jnp.int32)[None, :], 0), axis=1)
    kv_pool = jnp.take(all_pages, logical, axis=1)
    return (mixed, kv_pool)


def solution(mesh):
    placed = (P(("seq", "head"), None), P(), P(), P(), P(), P())
    return jax.shard_map(
        shards,
        mesh=mesh,
        in_specs=placed,
        out_specs=(P(("seq", "head"), None), P("head", "seq", None, None)),
        check_vma=False,
    )
```

```python
import functools

import jax
import jax.numpy as jnp
from jax import lax
from jax.experimental import pallas as pl
from jax.experimental.pallas import tpu as pltpu
from jax.sharding import PartitionSpec as P

KVH = 8
HD = 64
PAGE = 16
QPK = 4
TQ = 256
BK = 512
INTERPRET = False


def attention_kernel(seg_sm, base_sm, q_ref, kv_ref, qseg_ref, qidx_ref, kseg_ref,
                     o_ref, m_sc, l_sc, acc_sc):
    qi = pl.program_id(0)
    ki = pl.program_id(1)
    groups = q_ref.shape[0]
    tq = q_ref.shape[1] // QPK
    bk = kv_ref.shape[1]

    @pl.when(ki == 0)
    def _():
        m_sc[...] = jnp.full(m_sc.shape, -1e30, jnp.float32)
        l_sc[...] = jnp.zeros(l_sc.shape, jnp.float32)
        acc_sc[...] = jnp.zeros(acc_sc.shape, jnp.float32)

    q_first = base_sm[0] + qi * tq
    q_last = q_first + tq - 1
    k_first = ki * bk
    k_last = k_first + bk - 1
    active = (k_first <= q_last) & (seg_sm[k_first] <= seg_sm[q_last]) & (seg_sm[k_last] >= seg_sm[q_first])

    @pl.when(active)
    def _():
        kidx = k_first + lax.broadcasted_iota(jnp.int32, (1, bk), 1)
        qidx = qidx_ref[...]
        allowed = ((kseg_ref[...] == qseg_ref[...]) & (kidx <= qidx)) | (kidx == qidx)
        for g in range(groups):
            scores = lax.dot_general(
                q_ref[g], kv_ref[g], (((1,), (1,)), ((), ())), preferred_element_type=jnp.float32
            ) * 0.015625
            masked = jnp.where(allowed, scores, -1e30)
            m_old = m_sc[g]
            m_new = jnp.maximum(m_old, jnp.max(masked, axis=1, keepdims=True))
            m_row = jnp.where(m_new == -1e30, 0.0, m_new)
            weights = jnp.exp(masked - m_row)
            factor = jnp.exp(m_old - m_new)
            l_sc[g] = l_sc[g] * factor + jnp.sum(weights, axis=1, keepdims=True)
            update = jnp.dot(weights.astype(jnp.bfloat16), kv_ref[g], preferred_element_type=jnp.float32)
            acc_sc[g] = acc_sc[g] * factor + update
            m_sc[g] = m_new

    @pl.when(ki == pl.num_programs(1) - 1)
    def _():
        for g in range(groups):
            for c in range(QPK):
                lo = (g * QPK + c) * HD
                part = acc_sc[g, c * tq:(c + 1) * tq, HD:] / l_sc[g, c * tq:(c + 1) * tq]
                o_ref[:, lo:lo + HD] = part.astype(o_ref.dtype)


def attend(queries, keyvals_all, seg_ids, live, first_row):
    group_rows, groups = queries.shape[:2]
    tokens = keyvals_all.shape[1]
    tq = min(TQ, group_rows)
    nq = group_rows // tq
    bk = min(BK, tokens)
    nk = tokens // bk
    rows = QPK * tq
    q = queries.reshape(nq, tq, groups, QPK, HD).transpose(0, 2, 3, 1, 4).reshape(nq, groups, rows, HD)
    q = jnp.concatenate([q, jnp.zeros_like(q)], axis=-1)
    tok = first_row + jnp.arange(group_rows, dtype=jnp.int32)
    seg_here = lax.dynamic_slice_in_dim(seg_ids, first_row, group_rows, 0)

    def column(x):
        return jnp.broadcast_to(x.reshape(nq, 1, tq), (nq, QPK, tq)).reshape(nq, rows, 1)

    qidx = column(tok)
    qseg = column(seg_here)
    kseg = jnp.where(live == 1, seg_ids, -1).reshape(1, tokens)
    base = jnp.reshape(first_row, (1,)).astype(jnp.int32)

    def kmap(qi, ki, seg_sm, base_sm):
        return jnp.minimum(ki, (base_sm[0] + qi * tq + tq - 1) // bk)

    grid_spec = pltpu.PrefetchScalarGridSpec(
        num_scalar_prefetch=2,
        grid=(nq, nk),
        in_specs=[
            pl.BlockSpec((None, groups, rows, 2 * HD), lambda qi, ki, s, b: (qi, 0, 0, 0)),
            pl.BlockSpec((groups, bk, 2 * HD), lambda qi, ki, s, b: (0, kmap(qi, ki, s, b), 0)),
            pl.BlockSpec((None, rows, 1), lambda qi, ki, s, b: (qi, 0, 0)),
            pl.BlockSpec((None, rows, 1), lambda qi, ki, s, b: (qi, 0, 0)),
            pl.BlockSpec((1, bk), lambda qi, ki, s, b: (0, kmap(qi, ki, s, b))),
        ],
        out_specs=pl.BlockSpec((tq, groups * QPK * HD), lambda qi, ki, s, b: (qi, 0)),
        scratch_shapes=[
            pltpu.VMEM((groups, rows, 1), jnp.float32),
            pltpu.VMEM((groups, rows, 1), jnp.float32),
            pltpu.VMEM((groups, rows, 2 * HD), jnp.float32),
        ],
    )
    return pl.pallas_call(
        attention_kernel,
        out_shape=jax.ShapeDtypeStruct((group_rows, groups * QPK * HD), jnp.bfloat16),
        grid_spec=grid_spec,
        compiler_params=pltpu.CompilerParams(dimension_semantics=("arbitrary", "arbitrary")),
        interpret=INTERPRET,
    )(seg_ids, base, q, keyvals_all, qseg, qidx, kseg)


def exchange(chunks, heads_n, head_at):
    got = [lax.dynamic_index_in_dim(chunks, head_at, 0, keepdims=False)]
    for d in range(1, heads_n):
        mine = lax.dynamic_index_in_dim(chunks, (head_at + d) % heads_n, 0, keepdims=False)
        pairs = [(i, (i + d) % heads_n) for i in range(heads_n)]
        got.append(lax.ppermute(mine, "head", pairs))
    return got


def shards(hidden, w_qkv, w_out, seg_ids, live, page_table):
    heads_n = lax.axis_size("head")
    head_at = lax.axis_index("head")
    seq_at = lax.axis_index("seq")
    groups_here = KVH // heads_n
    per_group = (QPK + 2) * HD
    columns = groups_here * per_group
    local = jnp.dot(hidden, w_qkv, preferred_element_type=jnp.float32).astype(jnp.bfloat16)
    own_rows = local.shape[0]
    local = local.reshape(own_rows, heads_n, groups_here, QPK + 2, HD)
    kv_local = local[:, :, :, QPK:].reshape(own_rows, heads_n, groups_here, 2 * HD).transpose(1, 2, 0, 3)
    kv_got = exchange(kv_local, heads_n, head_at)
    kv_by_shift = jnp.stack(kv_got, axis=0)
    shift_of = (head_at - jnp.arange(heads_n, dtype=jnp.int32)) % heads_n
    kv_by_src = jnp.take(kv_by_shift, shift_of, axis=0)
    group_rows = own_rows * heads_n
    keyvals = kv_by_src.transpose(1, 0, 2, 3).reshape(groups_here, group_rows, 2 * HD)
    piece = lax.all_gather(keyvals, "seq", axis=1, tiled=True)
    q_local = local[:, :, :, :QPK].reshape(own_rows, heads_n, groups_here * QPK * HD)
    q_group = lax.all_to_all(q_local, "head", split_axis=1, concat_axis=0, tiled=True)
    queries = q_group.reshape(group_rows, groups_here, QPK, HD)
    first_row = (seq_at * group_rows).astype(jnp.int32)
    attended = attend(queries, piece, seg_ids, live, first_row)
    width = attended.shape[1]
    att_got = exchange(attended.reshape(heads_n, own_rows, width), heads_n, head_at)
    total = None
    for d in range(heads_n):
        src_head = (head_at - d) % heads_n
        w_rows = lax.dynamic_slice_in_dim(w_out, src_head * width, width, 0)
        partial = jnp.dot(att_got[d], w_rows, preferred_element_type=jnp.float32)
        total = partial if total is None else total + partial
    mixed = total.astype(jnp.bfloat16)
    pages_n = page_table.shape[0]
    page_count = pages_n // lax.axis_size("seq")
    all_pages = piece.reshape(groups_here, pages_n, PAGE, 2 * HD)
    wanted = seq_at * page_count + jnp.arange(page_count, dtype=jnp.int32)
    hits = page_table[None, :] == wanted[:, None]
    logical = jnp.sum(jnp.where(hits, jnp.arange(pages_n, dtype=jnp.int32)[None, :], 0), axis=1)
    kv_pool = jnp.take(all_pages, logical, axis=1)
    return (mixed, kv_pool)


def solution(mesh):
    placed = (P(("seq", "head"), None), P(), P(), P(), P(), P())
    return jax.shard_map(
        shards,
        mesh=mesh,
        in_specs=placed,
        out_specs=(P(("seq", "head"), None), P("head", "seq", None, None)),
        check_vma=False,
    )
```

```python
import functools

import jax
import jax.numpy as jnp
from jax import lax
from jax.experimental import pallas as pl
from jax.experimental.pallas import tpu as pltpu
from jax.sharding import PartitionSpec as P

KVH = 8
HD = 64
PAGE = 16
QPK = 4
TQ = 256
BK = 512
INTERPRET = False


def attention_kernel(seg_sm, base_sm, q_ref, kv_ref, qseg_ref, qidx_ref, kseg_ref,
                     o_ref, m_sc, l_sc, acc_sc):
    qi = pl.program_id(0)
    ki = pl.program_id(1)
    groups = q_ref.shape[0]
    tq = q_ref.shape[1] // QPK
    bk = kv_ref.shape[1]

    @pl.when(ki == 0)
    def _():
        m_sc[...] = jnp.full(m_sc.shape, -1e30, jnp.float32)
        l_sc[...] = jnp.zeros(l_sc.shape, jnp.float32)
        acc_sc[...] = jnp.zeros(acc_sc.shape, jnp.float32)

    q_first = base_sm[0] + qi * tq
    q_last = q_first + tq - 1
    k_first = ki * bk
    k_last = k_first + bk - 1
    active = (k_first <= q_last) & (seg_sm[k_first] <= seg_sm[q_last]) & (seg_sm[k_last] >= seg_sm[q_first])

    interior = (k_last < q_first) & (seg_sm[k_first] == seg_sm[q_last])

    def accumulate(allowed):
        for g in range(groups):
            scores = lax.dot_general(
                q_ref[g], kv_ref[g], (((1,), (1,)), ((), ())), preferred_element_type=jnp.float32
            ) * 0.015625
            masked = jnp.where(allowed, scores, -1e30)
            m_old = m_sc[g]
            m_new = jnp.maximum(m_old, jnp.max(masked, axis=1, keepdims=True))
            m_row = jnp.where(m_new == -1e30, 0.0, m_new)
            weights = jnp.exp(masked - m_row)
            factor = jnp.exp(m_old - m_new)
            l_sc[g] = l_sc[g] * factor + jnp.sum(weights, axis=1, keepdims=True)
            update = jnp.dot(weights.astype(jnp.bfloat16), kv_ref[g], preferred_element_type=jnp.float32)
            acc_sc[g] = acc_sc[g] * factor + update
            m_sc[g] = m_new

    @pl.when(active & interior)
    def _():
        accumulate(kseg_ref[...] == seg_sm[q_last])

    @pl.when(active & jnp.logical_not(interior))
    def _():
        kidx = k_first + lax.broadcasted_iota(jnp.int32, (1, bk), 1)
        qidx = qidx_ref[...]
        accumulate(((kseg_ref[...] == qseg_ref[...]) & (kidx <= qidx)) | (kidx == qidx))

    @pl.when(ki == pl.num_programs(1) - 1)
    def _():
        for g in range(groups):
            for c in range(QPK):
                lo = (g * QPK + c) * HD
                part = acc_sc[g, c * tq:(c + 1) * tq, HD:] / l_sc[g, c * tq:(c + 1) * tq]
                o_ref[:, lo:lo + HD] = part.astype(o_ref.dtype)


def attend(queries, keyvals_all, seg_ids, live, first_row):
    group_rows, groups = queries.shape[:2]
    tokens = keyvals_all.shape[1]
    tq = min(TQ, group_rows)
    nq = group_rows // tq
    bk = min(BK, tokens)
    nk = tokens // bk
    rows = QPK * tq
    q = queries.reshape(nq, tq, groups, QPK, HD).transpose(0, 2, 3, 1, 4).reshape(nq, groups, rows, HD)
    q = jnp.concatenate([q, jnp.zeros_like(q)], axis=-1)
    tok = first_row + jnp.arange(group_rows, dtype=jnp.int32)
    seg_here = lax.dynamic_slice_in_dim(seg_ids, first_row, group_rows, 0)

    def column(x):
        return jnp.broadcast_to(x.reshape(nq, 1, tq), (nq, QPK, tq)).reshape(nq, rows, 1)

    qidx = column(tok)
    qseg = column(seg_here)
    kseg = jnp.where(live == 1, seg_ids, -1).reshape(1, tokens)
    base = jnp.reshape(first_row, (1,)).astype(jnp.int32)

    def kmap(qi, ki, seg_sm, base_sm):
        return jnp.minimum(ki, (base_sm[0] + qi * tq + tq - 1) // bk)

    grid_spec = pltpu.PrefetchScalarGridSpec(
        num_scalar_prefetch=2,
        grid=(nq, nk),
        in_specs=[
            pl.BlockSpec((None, groups, rows, 2 * HD), lambda qi, ki, s, b: (qi, 0, 0, 0)),
            pl.BlockSpec((groups, bk, 2 * HD), lambda qi, ki, s, b: (0, kmap(qi, ki, s, b), 0)),
            pl.BlockSpec((None, rows, 1), lambda qi, ki, s, b: (qi, 0, 0)),
            pl.BlockSpec((None, rows, 1), lambda qi, ki, s, b: (qi, 0, 0)),
            pl.BlockSpec((1, bk), lambda qi, ki, s, b: (0, kmap(qi, ki, s, b))),
        ],
        out_specs=pl.BlockSpec((tq, groups * QPK * HD), lambda qi, ki, s, b: (qi, 0)),
        scratch_shapes=[
            pltpu.VMEM((groups, rows, 1), jnp.float32),
            pltpu.VMEM((groups, rows, 1), jnp.float32),
            pltpu.VMEM((groups, rows, 2 * HD), jnp.float32),
        ],
    )
    return pl.pallas_call(
        attention_kernel,
        out_shape=jax.ShapeDtypeStruct((group_rows, groups * QPK * HD), jnp.bfloat16),
        grid_spec=grid_spec,
        compiler_params=pltpu.CompilerParams(dimension_semantics=("arbitrary", "arbitrary")),
        interpret=INTERPRET,
    )(seg_ids, base, q, keyvals_all, qseg, qidx, kseg)


def exchange(chunks, heads_n, head_at):
    got = [lax.dynamic_index_in_dim(chunks, head_at, 0, keepdims=False)]
    for d in range(1, heads_n):
        mine = lax.dynamic_index_in_dim(chunks, (head_at + d) % heads_n, 0, keepdims=False)
        pairs = [(i, (i + d) % heads_n) for i in range(heads_n)]
        got.append(lax.ppermute(mine, "head", pairs))
    return got


def shards(hidden, w_qkv, w_out, seg_ids, live, page_table):
    heads_n = lax.axis_size("head")
    head_at = lax.axis_index("head")
    seq_at = lax.axis_index("seq")
    groups_here = KVH // heads_n
    per_group = (QPK + 2) * HD
    columns = groups_here * per_group
    local = jnp.dot(hidden, w_qkv, preferred_element_type=jnp.float32).astype(jnp.bfloat16)
    own_rows = local.shape[0]
    local = local.reshape(own_rows, heads_n, groups_here, QPK + 2, HD)
    kv_local = local[:, :, :, QPK:].reshape(own_rows, heads_n, groups_here, 2 * HD).transpose(1, 2, 0, 3)
    kv_got = exchange(kv_local, heads_n, head_at)
    kv_by_shift = jnp.stack(kv_got, axis=0)
    shift_of = (head_at - jnp.arange(heads_n, dtype=jnp.int32)) % heads_n
    kv_by_src = jnp.take(kv_by_shift, shift_of, axis=0)
    group_rows = own_rows * heads_n
    keyvals = kv_by_src.transpose(1, 0, 2, 3).reshape(groups_here, group_rows, 2 * HD)
    piece = lax.all_gather(keyvals, "seq", axis=1, tiled=True)
    q_local = local[:, :, :, :QPK].reshape(own_rows, heads_n, groups_here * QPK * HD)
    q_group = lax.all_to_all(q_local, "head", split_axis=1, concat_axis=0, tiled=True)
    queries = q_group.reshape(group_rows, groups_here, QPK, HD)
    first_row = (seq_at * group_rows).astype(jnp.int32)
    attended = attend(queries, piece, seg_ids, live, first_row)
    width = attended.shape[1]
    att_got = exchange(attended.reshape(heads_n, own_rows, width), heads_n, head_at)
    total = None
    for d in range(heads_n):
        src_head = (head_at - d) % heads_n
        w_rows = lax.dynamic_slice_in_dim(w_out, src_head * width, width, 0)
        partial = jnp.dot(att_got[d], w_rows, preferred_element_type=jnp.float32)
        total = partial if total is None else total + partial
    mixed = total.astype(jnp.bfloat16)
    pages_n = page_table.shape[0]
    page_count = pages_n // lax.axis_size("seq")
    all_pages = piece.reshape(groups_here, pages_n, PAGE, 2 * HD)
    wanted = seq_at * page_count + jnp.arange(page_count, dtype=jnp.int32)
    hits = page_table[None, :] == wanted[:, None]
    logical = jnp.sum(jnp.where(hits, jnp.arange(pages_n, dtype=jnp.int32)[None, :], 0), axis=1)
    kv_pool = jnp.take(all_pages, logical, axis=1)
    return (mixed, kv_pool)


def solution(mesh):
    placed = (P(("seq", "head"), None), P(), P(), P(), P(), P())
    return jax.shard_map(
        shards,
        mesh=mesh,
        in_specs=placed,
        out_specs=(P(("seq", "head"), None), P("head", "seq", None, None)),
        check_vma=False,
    )
```

```python
import functools

import jax
import jax.numpy as jnp
from jax import lax
from jax.experimental import pallas as pl
from jax.experimental.pallas import tpu as pltpu
from jax.sharding import PartitionSpec as P

KVH = 8
HD = 64
PAGE = 16
QPK = 4
TQ = 256
BK = 512
INTERPRET = False


def attention_kernel(seg_sm, base_sm, q_ref, kv_ref, qseg_ref, qidx_ref, kseg_ref,
                     o_ref, m_sc, l_sc, acc_sc):
    qi = pl.program_id(0)
    ki = pl.program_id(1)
    groups = q_ref.shape[0]
    tq = q_ref.shape[1] // QPK
    bk = kv_ref.shape[1]

    @pl.when(ki == 0)
    def _():
        m_sc[...] = jnp.full(m_sc.shape, -1e30, jnp.float32)
        l_sc[...] = jnp.zeros(l_sc.shape, jnp.float32)
        acc_sc[...] = jnp.zeros(acc_sc.shape, jnp.float32)

    q_first = base_sm[0] + qi * tq
    q_last = q_first + tq - 1
    k_first = ki * bk
    k_last = k_first + bk - 1
    active = (k_first <= q_last) & (seg_sm[k_first] <= seg_sm[q_last]) & (seg_sm[k_last] >= seg_sm[q_first])

    @pl.when(active)
    def _():
        kidx = k_first + lax.broadcasted_iota(jnp.int32, (1, bk), 1)
        qidx = qidx_ref[...]
        allowed = ((kseg_ref[...] == qseg_ref[...]) & (kidx <= qidx)) | (kidx == qidx)
        for g in range(groups):
            scores = lax.dot_general(
                q_ref[g], kv_ref[g], (((1,), (1,)), ((), ())), preferred_element_type=jnp.float32
            ) * 0.015625
            masked = jnp.where(allowed, scores, -1e30)
            m_old = m_sc[g]
            m_new = jnp.maximum(m_old, jnp.max(masked, axis=1, keepdims=True))
            m_row = jnp.where(m_new == -1e30, 0.0, m_new)
            weights = jnp.exp(masked - m_row)
            factor = jnp.exp(m_old - m_new)
            l_sc[g] = l_sc[g] * factor + jnp.sum(weights, axis=1, keepdims=True)
            update = jnp.dot(weights.astype(jnp.bfloat16), kv_ref[g], preferred_element_type=jnp.float32)
            acc_sc[g] = acc_sc[g] * factor + update
            m_sc[g] = m_new

    @pl.when(ki == pl.num_programs(1) - 1)
    def _():
        for g in range(groups):
            for c in range(QPK):
                lo = (g * QPK + c) * HD
                part = acc_sc[g, c * tq:(c + 1) * tq, HD:] / l_sc[g, c * tq:(c + 1) * tq]
                o_ref[:, lo:lo + HD] = part.astype(o_ref.dtype)


def attend(queries, keyvals_all, seg_ids, live, first_row):
    group_rows, groups = queries.shape[:2]
    tokens = keyvals_all.shape[1]
    tq = min(TQ, group_rows)
    nq = group_rows // tq
    bk = min(BK, tokens)
    nk = tokens // bk
    rows = QPK * tq
    q = queries.reshape(nq, tq, groups, QPK, HD).transpose(0, 2, 3, 1, 4).reshape(nq, groups, rows, HD)
    q = jnp.concatenate([q, jnp.zeros_like(q)], axis=-1)
    tok = first_row + jnp.arange(group_rows, dtype=jnp.int32)
    seg_here = lax.dynamic_slice_in_dim(seg_ids, first_row, group_rows, 0)

    def column(x):
        return jnp.broadcast_to(x.reshape(nq, 1, tq), (nq, QPK, tq)).reshape(nq, rows, 1)

    qidx = column(tok)
    qseg = column(seg_here)
    kseg = jnp.where(live == 1, seg_ids, -1).reshape(1, tokens)
    base = jnp.reshape(first_row, (1,)).astype(jnp.int32)

    def kmap(qi, ki, seg_sm, base_sm):
        return jnp.minimum(ki, (base_sm[0] + qi * tq + tq - 1) // bk)

    grid_spec = pltpu.PrefetchScalarGridSpec(
        num_scalar_prefetch=2,
        grid=(nq, nk),
        in_specs=[
            pl.BlockSpec((None, groups, rows, 2 * HD), lambda qi, ki, s, b: (qi, 0, 0, 0)),
            pl.BlockSpec((groups, bk, 2 * HD), lambda qi, ki, s, b: (0, kmap(qi, ki, s, b), 0)),
            pl.BlockSpec((None, rows, 1), lambda qi, ki, s, b: (qi, 0, 0)),
            pl.BlockSpec((None, rows, 1), lambda qi, ki, s, b: (qi, 0, 0)),
            pl.BlockSpec((1, bk), lambda qi, ki, s, b: (0, kmap(qi, ki, s, b))),
        ],
        out_specs=pl.BlockSpec((tq, groups * QPK * HD), lambda qi, ki, s, b: (qi, 0)),
        scratch_shapes=[
            pltpu.VMEM((groups, rows, 1), jnp.float32),
            pltpu.VMEM((groups, rows, 1), jnp.float32),
            pltpu.VMEM((groups, rows, 2 * HD), jnp.float32),
        ],
    )
    return pl.pallas_call(
        attention_kernel,
        out_shape=jax.ShapeDtypeStruct((group_rows, groups * QPK * HD), jnp.bfloat16),
        grid_spec=grid_spec,
        compiler_params=pltpu.CompilerParams(dimension_semantics=("arbitrary", "arbitrary")),
        interpret=INTERPRET,
    )(seg_ids, base, q, keyvals_all, qseg, qidx, kseg)


def exchange(chunks, heads_n, head_at):
    got = [lax.dynamic_index_in_dim(chunks, head_at, 0, keepdims=False)]
    for d in range(1, heads_n):
        mine = lax.dynamic_index_in_dim(chunks, (head_at + d) % heads_n, 0, keepdims=False)
        pairs = [(i, (i + d) % heads_n) for i in range(heads_n)]
        got.append(lax.ppermute(mine, "head", pairs))
    return got


def shards(hidden, w_qkv, w_out, seg_ids, live, page_table):
    heads_n = lax.axis_size("head")
    head_at = lax.axis_index("head")
    seq_at = lax.axis_index("seq")
    groups_here = KVH // heads_n
    per_group = (QPK + 2) * HD
    columns = groups_here * per_group
    local = jnp.dot(hidden, w_qkv, preferred_element_type=jnp.float32).astype(jnp.bfloat16)
    own_rows = local.shape[0]
    local = local.reshape(own_rows, heads_n, groups_here, QPK + 2, HD)
    kv_local = local[:, :, :, QPK:].reshape(own_rows, heads_n, groups_here, 2 * HD).transpose(1, 2, 0, 3)
    kv_got = exchange(kv_local, heads_n, head_at)
    kv_by_shift = jnp.stack(kv_got, axis=0)
    shift_of = (head_at - jnp.arange(heads_n, dtype=jnp.int32)) % heads_n
    kv_by_src = jnp.take(kv_by_shift, shift_of, axis=0)
    group_rows = own_rows * heads_n
    keyvals = kv_by_src.transpose(1, 0, 2, 3).reshape(groups_here, group_rows, 2 * HD)
    piece = lax.all_gather(keyvals, "seq", axis=1, tiled=True)
    q_local = local[:, :, :, :QPK].reshape(own_rows, heads_n, groups_here * QPK * HD).transpose(1, 0, 2)
    q_by_shift = jnp.stack(exchange(q_local, heads_n, head_at), axis=0)
    q_by_src = jnp.take(q_by_shift, shift_of, axis=0)
    queries = q_by_src.reshape(group_rows, groups_here, QPK, HD)
    first_row = (seq_at * group_rows).astype(jnp.int32)
    attended = attend(queries, piece, seg_ids, live, first_row)
    width = attended.shape[1]
    att_got = exchange(attended.reshape(heads_n, own_rows, width), heads_n, head_at)
    total = None
    for d in range(heads_n):
        src_head = (head_at - d) % heads_n
        w_rows = lax.dynamic_slice_in_dim(w_out, src_head * width, width, 0)
        partial = jnp.dot(att_got[d], w_rows, preferred_element_type=jnp.float32)
        total = partial if total is None else total + partial
    mixed = total.astype(jnp.bfloat16)
    pages_n = page_table.shape[0]
    page_count = pages_n // lax.axis_size("seq")
    all_pages = piece.reshape(groups_here, pages_n, PAGE, 2 * HD)
    wanted = seq_at * page_count + jnp.arange(page_count, dtype=jnp.int32)
    hits = page_table[None, :] == wanted[:, None]
    logical = jnp.sum(jnp.where(hits, jnp.arange(pages_n, dtype=jnp.int32)[None, :], 0), axis=1)
    kv_pool = jnp.take(all_pages, logical, axis=1)
    return (mixed, kv_pool)


def solution(mesh):
    placed = (P(("seq", "head"), None), P(), P(), P(), P(), P())
    return jax.shard_map(
        shards,
        mesh=mesh,
        in_specs=placed,
        out_specs=(P(("seq", "head"), None), P("head", "seq", None, None)),
        check_vma=False,
    )
```

```python
import functools

import jax
import jax.numpy as jnp
from jax import lax
from jax.experimental import pallas as pl
from jax.experimental.pallas import tpu as pltpu
from jax.sharding import PartitionSpec as P

KVH = 8
HD = 64
PAGE = 16
QPK = 4
TQ = 512
BK = 512
INTERPRET = False


def attention_kernel(seg_sm, base_sm, q_ref, kv_ref, qseg_ref, qidx_ref, kseg_ref,
                     o_ref, m_sc, l_sc, acc_sc):
    qi = pl.program_id(0)
    ki = pl.program_id(1)
    groups = q_ref.shape[0]
    tq = q_ref.shape[1] // QPK
    bk = kv_ref.shape[1]

    @pl.when(ki == 0)
    def _():
        m_sc[...] = jnp.full(m_sc.shape, -1e30, jnp.float32)
        l_sc[...] = jnp.zeros(l_sc.shape, jnp.float32)
        acc_sc[...] = jnp.zeros(acc_sc.shape, jnp.float32)

    q_first = base_sm[0] + qi * tq
    q_last = q_first + tq - 1
    k_first = ki * bk
    k_last = k_first + bk - 1
    active = (k_first <= q_last) & (seg_sm[k_first] <= seg_sm[q_last]) & (seg_sm[k_last] >= seg_sm[q_first])

    @pl.when(active)
    def _():
        kidx = k_first + lax.broadcasted_iota(jnp.int32, (1, bk), 1)
        qidx = qidx_ref[...]
        allowed = ((kseg_ref[...] == qseg_ref[...]) & (kidx <= qidx)) | (kidx == qidx)
        for g in range(groups):
            scores = lax.dot_general(
                q_ref[g], kv_ref[g], (((1,), (1,)), ((), ())), preferred_element_type=jnp.float32
            ) * 0.015625
            masked = jnp.where(allowed, scores, -1e30)
            m_old = m_sc[g]
            m_new = jnp.maximum(m_old, jnp.max(masked, axis=1, keepdims=True))
            m_row = jnp.where(m_new == -1e30, 0.0, m_new)
            weights = jnp.exp(masked - m_row)
            factor = jnp.exp(m_old - m_new)
            l_sc[g] = l_sc[g] * factor + jnp.sum(weights, axis=1, keepdims=True)
            update = jnp.dot(weights.astype(jnp.bfloat16), kv_ref[g], preferred_element_type=jnp.float32)
            acc_sc[g] = acc_sc[g] * factor + update
            m_sc[g] = m_new

    @pl.when(ki == pl.num_programs(1) - 1)
    def _():
        for g in range(groups):
            for c in range(QPK):
                lo = (g * QPK + c) * HD
                part = acc_sc[g, c * tq:(c + 1) * tq, HD:] / l_sc[g, c * tq:(c + 1) * tq]
                o_ref[:, lo:lo + HD] = part.astype(o_ref.dtype)


def attend(queries, keyvals_all, seg_ids, live, first_row):
    group_rows, groups = queries.shape[:2]
    tokens = keyvals_all.shape[1]
    tq = min(TQ, group_rows)
    nq = group_rows // tq
    bk = min(BK, tokens)
    nk = tokens // bk
    rows = QPK * tq
    q = queries.reshape(nq, tq, groups, QPK, HD).transpose(0, 2, 3, 1, 4).reshape(nq, groups, rows, HD)
    q = jnp.concatenate([q, jnp.zeros_like(q)], axis=-1)
    tok = first_row + jnp.arange(group_rows, dtype=jnp.int32)
    seg_here = lax.dynamic_slice_in_dim(seg_ids, first_row, group_rows, 0)

    def column(x):
        return jnp.broadcast_to(x.reshape(nq, 1, tq), (nq, QPK, tq)).reshape(nq, rows, 1)

    qidx = column(tok)
    qseg = column(seg_here)
    kseg = jnp.where(live == 1, seg_ids, -1).reshape(1, tokens)
    base = jnp.reshape(first_row, (1,)).astype(jnp.int32)

    def kmap(qi, ki, seg_sm, base_sm):
        return jnp.minimum(ki, (base_sm[0] + qi * tq + tq - 1) // bk)

    grid_spec = pltpu.PrefetchScalarGridSpec(
        num_scalar_prefetch=2,
        grid=(nq, nk),
        in_specs=[
            pl.BlockSpec((None, groups, rows, 2 * HD), lambda qi, ki, s, b: (qi, 0, 0, 0)),
            pl.BlockSpec((groups, bk, 2 * HD), lambda qi, ki, s, b: (0, kmap(qi, ki, s, b), 0)),
            pl.BlockSpec((None, rows, 1), lambda qi, ki, s, b: (qi, 0, 0)),
            pl.BlockSpec((None, rows, 1), lambda qi, ki, s, b: (qi, 0, 0)),
            pl.BlockSpec((1, bk), lambda qi, ki, s, b: (0, kmap(qi, ki, s, b))),
        ],
        out_specs=pl.BlockSpec((tq, groups * QPK * HD), lambda qi, ki, s, b: (qi, 0)),
        scratch_shapes=[
            pltpu.VMEM((groups, rows, 1), jnp.float32),
            pltpu.VMEM((groups, rows, 1), jnp.float32),
            pltpu.VMEM((groups, rows, 2 * HD), jnp.float32),
        ],
    )
    return pl.pallas_call(
        attention_kernel,
        out_shape=jax.ShapeDtypeStruct((group_rows, groups * QPK * HD), jnp.bfloat16),
        grid_spec=grid_spec,
        compiler_params=pltpu.CompilerParams(dimension_semantics=("arbitrary", "arbitrary")),
        interpret=INTERPRET,
    )(seg_ids, base, q, keyvals_all, qseg, qidx, kseg)


def exchange(chunks, heads_n, head_at):
    got = [lax.dynamic_index_in_dim(chunks, head_at, 0, keepdims=False)]
    for d in range(1, heads_n):
        mine = lax.dynamic_index_in_dim(chunks, (head_at + d) % heads_n, 0, keepdims=False)
        pairs = [(i, (i + d) % heads_n) for i in range(heads_n)]
        got.append(lax.ppermute(mine, "head", pairs))
    return got


def shards(hidden, w_qkv, w_out, seg_ids, live, page_table):
    heads_n = lax.axis_size("head")
    head_at = lax.axis_index("head")
    seq_at = lax.axis_index("seq")
    groups_here = KVH // heads_n
    per_group = (QPK + 2) * HD
    columns = groups_here * per_group
    local = jnp.dot(hidden, w_qkv, preferred_element_type=jnp.float32).astype(jnp.bfloat16)
    own_rows = local.shape[0]
    local = local.reshape(own_rows, heads_n, groups_here, QPK + 2, HD)
    kv_local = local[:, :, :, QPK:].reshape(own_rows, heads_n, groups_here, 2 * HD).transpose(1, 2, 0, 3)
    kv_got = exchange(kv_local, heads_n, head_at)
    kv_by_shift = jnp.stack(kv_got, axis=0)
    shift_of = (head_at - jnp.arange(heads_n, dtype=jnp.int32)) % heads_n
    kv_by_src = jnp.take(kv_by_shift, shift_of, axis=0)
    group_rows = own_rows * heads_n
    keyvals = kv_by_src.transpose(1, 0, 2, 3).reshape(groups_here, group_rows, 2 * HD)
    piece = lax.all_gather(keyvals, "seq", axis=1, tiled=True)
    q_local = local[:, :, :, :QPK].reshape(own_rows, heads_n, groups_here * QPK * HD).transpose(1, 0, 2)
    q_by_shift = jnp.stack(exchange(q_local, heads_n, head_at), axis=0)
    q_by_src = jnp.take(q_by_shift, shift_of, axis=0)
    queries = q_by_src.reshape(group_rows, groups_here, QPK, HD)
    first_row = (seq_at * group_rows).astype(jnp.int32)
    attended = attend(queries, piece, seg_ids, live, first_row)
    width = attended.shape[1]
    att_got = exchange(attended.reshape(heads_n, own_rows, width), heads_n, head_at)
    total = None
    for d in range(heads_n):
        src_head = (head_at - d) % heads_n
        w_rows = lax.dynamic_slice_in_dim(w_out, src_head * width, width, 0)
        partial = jnp.dot(att_got[d], w_rows, preferred_element_type=jnp.float32)
        total = partial if total is None else total + partial
    mixed = total.astype(jnp.bfloat16)
    pages_n = page_table.shape[0]
    page_count = pages_n // lax.axis_size("seq")
    all_pages = piece.reshape(groups_here, pages_n, PAGE, 2 * HD)
    wanted = seq_at * page_count + jnp.arange(page_count, dtype=jnp.int32)
    hits = page_table[None, :] == wanted[:, None]
    logical = jnp.sum(jnp.where(hits, jnp.arange(pages_n, dtype=jnp.int32)[None, :], 0), axis=1)
    kv_pool = jnp.take(all_pages, logical, axis=1)
    return (mixed, kv_pool)


def solution(mesh):
    placed = (P(("seq", "head"), None), P(), P(), P(), P(), P())
    return jax.shard_map(
        shards,
        mesh=mesh,
        in_specs=placed,
        out_specs=(P(("seq", "head"), None), P("head", "seq", None, None)),
        check_vma=False,
    )
```

```python
import functools

import jax
import jax.numpy as jnp
from jax import lax
from jax.experimental import pallas as pl
from jax.experimental.pallas import tpu as pltpu
from jax.sharding import PartitionSpec as P

KVH = 8
HD = 64
PAGE = 16
QPK = 4
TQ = 512
BK = 512
INTERPRET = False


def attention_kernel(seg_sm, base_sm, q_ref, kv_ref, qseg_ref, qidx_ref, kseg_ref,
                     o_ref, m_sc, l_sc, acc_sc):
    qi = pl.program_id(0)
    ki = pl.program_id(1)
    groups = q_ref.shape[0]
    tq = q_ref.shape[1] // QPK
    bk = kv_ref.shape[1]

    @pl.when(ki == 0)
    def _():
        m_sc[...] = jnp.full(m_sc.shape, -1e30, jnp.float32)
        l_sc[...] = jnp.zeros(l_sc.shape, jnp.float32)
        acc_sc[...] = jnp.zeros(acc_sc.shape, jnp.float32)

    q_first = base_sm[0] + qi * tq
    q_last = q_first + tq - 1
    k_first = ki * bk
    k_last = k_first + bk - 1
    active = (k_first <= q_last) & (seg_sm[k_first] <= seg_sm[q_last]) & (seg_sm[k_last] >= seg_sm[q_first])

    @pl.when(active)
    def _():
        kidx = k_first + lax.broadcasted_iota(jnp.int32, (1, bk), 1)
        qidx = qidx_ref[...]
        allowed = ((kseg_ref[...] == qseg_ref[...]) & (kidx <= qidx)) | (kidx == qidx)
        for g in range(groups):
            scores = lax.dot_general(
                q_ref[g], kv_ref[g], (((1,), (1,)), ((), ())), preferred_element_type=jnp.float32
            ) * 0.015625
            masked = jnp.where(allowed, scores, -1e30)
            m_old = m_sc[g]
            m_new = jnp.maximum(m_old, jnp.max(masked, axis=1, keepdims=True))
            m_row = jnp.where(m_new == -1e30, 0.0, m_new)
            weights = jnp.exp(masked - m_row)
            factor = jnp.exp(m_old - m_new)
            l_sc[g] = l_sc[g] * factor + jnp.sum(weights, axis=1, keepdims=True)
            update = jnp.dot(weights.astype(jnp.bfloat16), kv_ref[g], preferred_element_type=jnp.float32)
            acc_sc[g] = acc_sc[g] * factor + update
            m_sc[g] = m_new

    @pl.when(ki == pl.num_programs(1) - 1)
    def _():
        for g in range(groups):
            for c in range(QPK):
                lo = (g * QPK + c) * HD
                part = acc_sc[g, c * tq:(c + 1) * tq, HD:] / l_sc[g, c * tq:(c + 1) * tq]
                o_ref[:, lo:lo + HD] = part.astype(o_ref.dtype)


def attend(queries, keyvals_all, seg_ids, live, first_row):
    group_rows, groups = queries.shape[:2]
    tokens = keyvals_all.shape[1]
    tq = min(TQ, group_rows)
    nq = group_rows // tq
    bk = min(BK, tokens)
    nk = tokens // bk
    rows = QPK * tq
    q = queries.reshape(nq, tq, groups, QPK, HD).transpose(0, 2, 3, 1, 4).reshape(nq, groups, rows, HD)
    q = jnp.concatenate([q, jnp.zeros_like(q)], axis=-1)
    tok = first_row + jnp.arange(group_rows, dtype=jnp.int32)
    seg_here = lax.dynamic_slice_in_dim(seg_ids, first_row, group_rows, 0)

    def column(x):
        return jnp.broadcast_to(x.reshape(nq, 1, tq), (nq, QPK, tq)).reshape(nq, rows, 1)

    qidx = column(tok)
    qseg = column(seg_here)
    kseg = jnp.where(live == 1, seg_ids, -1).reshape(1, tokens)
    base = jnp.reshape(first_row, (1,)).astype(jnp.int32)

    def kmap(qi, ki, seg_sm, base_sm):
        return jnp.minimum(ki, (base_sm[0] + qi * tq + tq - 1) // bk)

    grid_spec = pltpu.PrefetchScalarGridSpec(
        num_scalar_prefetch=2,
        grid=(nq, nk),
        in_specs=[
            pl.BlockSpec((None, groups, rows, 2 * HD), lambda qi, ki, s, b: (qi, 0, 0, 0)),
            pl.BlockSpec((groups, bk, 2 * HD), lambda qi, ki, s, b: (0, kmap(qi, ki, s, b), 0)),
            pl.BlockSpec((None, rows, 1), lambda qi, ki, s, b: (qi, 0, 0)),
            pl.BlockSpec((None, rows, 1), lambda qi, ki, s, b: (qi, 0, 0)),
            pl.BlockSpec((1, bk), lambda qi, ki, s, b: (0, kmap(qi, ki, s, b))),
        ],
        out_specs=pl.BlockSpec((tq, groups * QPK * HD), lambda qi, ki, s, b: (qi, 0)),
        scratch_shapes=[
            pltpu.VMEM((groups, rows, 1), jnp.float32),
            pltpu.VMEM((groups, rows, 1), jnp.float32),
            pltpu.VMEM((groups, rows, 2 * HD), jnp.float32),
        ],
    )
    return pl.pallas_call(
        attention_kernel,
        out_shape=jax.ShapeDtypeStruct((group_rows, groups * QPK * HD), jnp.bfloat16),
        grid_spec=grid_spec,
        compiler_params=pltpu.CompilerParams(dimension_semantics=("arbitrary", "arbitrary")),
        interpret=INTERPRET,
    )(seg_ids, base, q, keyvals_all, qseg, qidx, kseg)


def exchange(chunks, heads_n, head_at):
    got = [lax.dynamic_index_in_dim(chunks, head_at, 0, keepdims=False)]
    for d in range(1, heads_n):
        mine = lax.dynamic_index_in_dim(chunks, (head_at + d) % heads_n, 0, keepdims=False)
        pairs = [(i, (i + d) % heads_n) for i in range(heads_n)]
        got.append(lax.ppermute(mine, "head", pairs))
    return got


def shards(hidden, w_qkv, w_out, seg_ids, live, page_table):
    heads_n = lax.axis_size("head")
    head_at = lax.axis_index("head")
    seq_at = lax.axis_index("seq")
    groups_here = KVH // heads_n
    per_group = (QPK + 2) * HD
    columns = groups_here * per_group
    local = jnp.dot(hidden, w_qkv, preferred_element_type=jnp.float32).astype(jnp.bfloat16)
    own_rows = local.shape[0]
    local = local.reshape(own_rows, heads_n, groups_here, QPK + 2, HD)
    kv_local = local[:, :, :, QPK:].reshape(own_rows, heads_n, groups_here, 2 * HD).transpose(1, 2, 0, 3)
    kv_got = exchange(kv_local, heads_n, head_at)
    kv_by_shift = jnp.stack(kv_got, axis=0)
    shift_of = (head_at - jnp.arange(heads_n, dtype=jnp.int32)) % heads_n
    kv_by_src = jnp.take(kv_by_shift, shift_of, axis=0)
    group_rows = own_rows * heads_n
    keyvals = kv_by_src.transpose(1, 0, 2, 3).reshape(groups_here, group_rows, 2 * HD)
    pieces = [lax.all_gather(keyvals[g:g + 1], "seq", axis=1, tiled=True) for g in range(groups_here)]
    piece = jnp.concatenate(pieces, axis=0)
    q_local = local[:, :, :, :QPK].reshape(own_rows, heads_n, groups_here * QPK * HD).transpose(1, 0, 2)
    q_by_shift = jnp.stack(exchange(q_local, heads_n, head_at), axis=0)
    q_by_src = jnp.take(q_by_shift, shift_of, axis=0)
    queries = q_by_src.reshape(group_rows, groups_here, QPK, HD)
    first_row = (seq_at * group_rows).astype(jnp.int32)
    attended = jnp.concatenate(
        [attend(queries[:, g:g + 1], pieces[g], seg_ids, live, first_row) for g in range(groups_here)], axis=1
    )
    width = attended.shape[1]
    att_got = exchange(attended.reshape(heads_n, own_rows, width), heads_n, head_at)
    total = None
    for d in range(heads_n):
        src_head = (head_at - d) % heads_n
        w_rows = lax.dynamic_slice_in_dim(w_out, src_head * width, width, 0)
        partial = jnp.dot(att_got[d], w_rows, preferred_element_type=jnp.float32)
        total = partial if total is None else total + partial
    mixed = total.astype(jnp.bfloat16)
    pages_n = page_table.shape[0]
    page_count = pages_n // lax.axis_size("seq")
    all_pages = piece.reshape(groups_here, pages_n, PAGE, 2 * HD)
    wanted = seq_at * page_count + jnp.arange(page_count, dtype=jnp.int32)
    hits = page_table[None, :] == wanted[:, None]
    logical = jnp.sum(jnp.where(hits, jnp.arange(pages_n, dtype=jnp.int32)[None, :], 0), axis=1)
    kv_pool = jnp.take(all_pages, logical, axis=1)
    return (mixed, kv_pool)


def solution(mesh):
    placed = (P(("seq", "head"), None), P(), P(), P(), P(), P())
    return jax.shard_map(
        shards,
        mesh=mesh,
        in_specs=placed,
        out_specs=(P(("seq", "head"), None), P("head", "seq", None, None)),
        check_vma=False,
    )
```

```python
import functools

import jax
import jax.numpy as jnp
from jax import lax
from jax.experimental import pallas as pl
from jax.experimental.pallas import tpu as pltpu
from jax.sharding import PartitionSpec as P

KVH = 8
HD = 64
PAGE = 16
QPK = 4
TQ = 512
BK = 1024
INTERPRET = False


def attention_kernel(seg_sm, base_sm, q_ref, kv_ref, qseg_ref, qidx_ref, kseg_ref,
                     o_ref, m_sc, l_sc, acc_sc):
    qi = pl.program_id(0)
    ki = pl.program_id(1)
    groups = q_ref.shape[0]
    tq = q_ref.shape[1] // QPK
    bk = kv_ref.shape[1]

    @pl.when(ki == 0)
    def _():
        m_sc[...] = jnp.full(m_sc.shape, -1e30, jnp.float32)
        l_sc[...] = jnp.zeros(l_sc.shape, jnp.float32)
        acc_sc[...] = jnp.zeros(acc_sc.shape, jnp.float32)

    q_first = base_sm[0] + qi * tq
    q_last = q_first + tq - 1
    k_first = ki * bk
    k_last = k_first + bk - 1
    active = (k_first <= q_last) & (seg_sm[k_first] <= seg_sm[q_last]) & (seg_sm[k_last] >= seg_sm[q_first])

    @pl.when(active)
    def _():
        kidx = k_first + lax.broadcasted_iota(jnp.int32, (1, bk), 1)
        qidx = qidx_ref[...]
        allowed = ((kseg_ref[...] == qseg_ref[...]) & (kidx <= qidx)) | (kidx == qidx)
        for g in range(groups):
            scores = lax.dot_general(
                q_ref[g], kv_ref[g], (((1,), (1,)), ((), ())), preferred_element_type=jnp.float32
            ) * 0.015625
            masked = jnp.where(allowed, scores, -1e30)
            m_old = m_sc[g]
            m_new = jnp.maximum(m_old, jnp.max(masked, axis=1, keepdims=True))
            m_row = jnp.where(m_new == -1e30, 0.0, m_new)
            weights = jnp.exp(masked - m_row)
            factor = jnp.exp(m_old - m_new)
            l_sc[g] = l_sc[g] * factor + jnp.sum(weights, axis=1, keepdims=True)
            update = jnp.dot(weights.astype(jnp.bfloat16), kv_ref[g], preferred_element_type=jnp.float32)
            acc_sc[g] = acc_sc[g] * factor + update
            m_sc[g] = m_new

    @pl.when(ki == pl.num_programs(1) - 1)
    def _():
        for g in range(groups):
            for c in range(QPK):
                lo = (g * QPK + c) * HD
                part = acc_sc[g, c * tq:(c + 1) * tq, HD:] / l_sc[g, c * tq:(c + 1) * tq]
                o_ref[:, lo:lo + HD] = part.astype(o_ref.dtype)


def attend(queries, keyvals_all, seg_ids, live, first_row):
    group_rows, groups = queries.shape[:2]
    tokens = keyvals_all.shape[1]
    tq = min(TQ, group_rows)
    nq = group_rows // tq
    bk = min(BK, tokens)
    nk = tokens // bk
    rows = QPK * tq
    q = queries.reshape(nq, tq, groups, QPK, HD).transpose(0, 2, 3, 1, 4).reshape(nq, groups, rows, HD)
    q = jnp.concatenate([q, jnp.zeros_like(q)], axis=-1)
    tok = first_row + jnp.arange(group_rows, dtype=jnp.int32)
    seg_here = lax.dynamic_slice_in_dim(seg_ids, first_row, group_rows, 0)

    def column(x):
        return jnp.broadcast_to(x.reshape(nq, 1, tq), (nq, QPK, tq)).reshape(nq, rows, 1)

    qidx = column(tok)
    qseg = column(seg_here)
    kseg = jnp.where(live == 1, seg_ids, -1).reshape(1, tokens)
    base = jnp.reshape(first_row, (1,)).astype(jnp.int32)

    def kmap(qi, ki, seg_sm, base_sm):
        return jnp.minimum(ki, (base_sm[0] + qi * tq + tq - 1) // bk)

    grid_spec = pltpu.PrefetchScalarGridSpec(
        num_scalar_prefetch=2,
        grid=(nq, nk),
        in_specs=[
            pl.BlockSpec((None, groups, rows, 2 * HD), lambda qi, ki, s, b: (qi, 0, 0, 0)),
            pl.BlockSpec((groups, bk, 2 * HD), lambda qi, ki, s, b: (0, kmap(qi, ki, s, b), 0)),
            pl.BlockSpec((None, rows, 1), lambda qi, ki, s, b: (qi, 0, 0)),
            pl.BlockSpec((None, rows, 1), lambda qi, ki, s, b: (qi, 0, 0)),
            pl.BlockSpec((1, bk), lambda qi, ki, s, b: (0, kmap(qi, ki, s, b))),
        ],
        out_specs=pl.BlockSpec((tq, groups * QPK * HD), lambda qi, ki, s, b: (qi, 0)),
        scratch_shapes=[
            pltpu.VMEM((groups, rows, 1), jnp.float32),
            pltpu.VMEM((groups, rows, 1), jnp.float32),
            pltpu.VMEM((groups, rows, 2 * HD), jnp.float32),
        ],
    )
    return pl.pallas_call(
        attention_kernel,
        out_shape=jax.ShapeDtypeStruct((group_rows, groups * QPK * HD), jnp.bfloat16),
        grid_spec=grid_spec,
        compiler_params=pltpu.CompilerParams(dimension_semantics=("arbitrary", "arbitrary")),
        interpret=INTERPRET,
    )(seg_ids, base, q, keyvals_all, qseg, qidx, kseg)


def exchange(chunks, heads_n, head_at):
    got = [lax.dynamic_index_in_dim(chunks, head_at, 0, keepdims=False)]
    for d in range(1, heads_n):
        mine = lax.dynamic_index_in_dim(chunks, (head_at + d) % heads_n, 0, keepdims=False)
        pairs = [(i, (i + d) % heads_n) for i in range(heads_n)]
        got.append(lax.ppermute(mine, "head", pairs))
    return got


def shards(hidden, w_qkv, w_out, seg_ids, live, page_table):
    heads_n = lax.axis_size("head")
    head_at = lax.axis_index("head")
    seq_at = lax.axis_index("seq")
    groups_here = KVH // heads_n
    per_group = (QPK + 2) * HD
    columns = groups_here * per_group
    local = jnp.dot(hidden, w_qkv, preferred_element_type=jnp.float32).astype(jnp.bfloat16)
    own_rows = local.shape[0]
    local = local.reshape(own_rows, heads_n, groups_here, QPK + 2, HD)
    kv_local = local[:, :, :, QPK:].reshape(own_rows, heads_n, groups_here, 2 * HD).transpose(1, 2, 0, 3)
    kv_got = exchange(kv_local, heads_n, head_at)
    kv_by_shift = jnp.stack(kv_got, axis=0)
    shift_of = (head_at - jnp.arange(heads_n, dtype=jnp.int32)) % heads_n
    kv_by_src = jnp.take(kv_by_shift, shift_of, axis=0)
    group_rows = own_rows * heads_n
    keyvals = kv_by_src.transpose(1, 0, 2, 3).reshape(groups_here, group_rows, 2 * HD)
    piece = lax.all_gather(keyvals, "seq", axis=1, tiled=True)
    q_local = local[:, :, :, :QPK].reshape(own_rows, heads_n, groups_here * QPK * HD).transpose(1, 0, 2)
    q_by_shift = jnp.stack(exchange(q_local, heads_n, head_at), axis=0)
    q_by_src = jnp.take(q_by_shift, shift_of, axis=0)
    queries = q_by_src.reshape(group_rows, groups_here, QPK, HD)
    first_row = (seq_at * group_rows).astype(jnp.int32)
    attended = attend(queries, piece, seg_ids, live, first_row)
    width = attended.shape[1]
    att_got = exchange(attended.reshape(heads_n, own_rows, width), heads_n, head_at)
    total = None
    for d in range(heads_n):
        src_head = (head_at - d) % heads_n
        w_rows = lax.dynamic_slice_in_dim(w_out, src_head * width, width, 0)
        partial = jnp.dot(att_got[d], w_rows, preferred_element_type=jnp.float32)
        total = partial if total is None else total + partial
    mixed = total.astype(jnp.bfloat16)
    pages_n = page_table.shape[0]
    page_count = pages_n // lax.axis_size("seq")
    all_pages = piece.reshape(groups_here, pages_n, PAGE, 2 * HD)
    wanted = seq_at * page_count + jnp.arange(page_count, dtype=jnp.int32)
    hits = page_table[None, :] == wanted[:, None]
    logical = jnp.sum(jnp.where(hits, jnp.arange(pages_n, dtype=jnp.int32)[None, :], 0), axis=1)
    kv_pool = jnp.take(all_pages, logical, axis=1)
    return (mixed, kv_pool)


def solution(mesh):
    placed = (P(("seq", "head"), None), P(), P(), P(), P(), P())
    return jax.shard_map(
        shards,
        mesh=mesh,
        in_specs=placed,
        out_specs=(P(("seq", "head"), None), P("head", "seq", None, None)),
        check_vma=False,
    )
```
